256 devices in a mesh: grp: 2 (over core), req: 128 (over y, z, x).
Axes of the slice: x: 4, y: 4, z: 8, core: 2. Of those that a mesh axis runs over, the one named last changes fastest.
Arguments:
- new_qkv: bfloat16 [1024, 32, 3840], P(('grp', 'req')), parts along dimension 0, may hold values from -5 to 5
- cache_kv: bfloat16 [1024, 32, 2560], P(('grp', 'req')), parts along dimension 0, may hold values from -5 to 5
- resid: bfloat16 [1024, 32, 1280], P(('grp', 'req')), parts along dimension 0, may hold values from -6 to 6
- span_len: int32 [1024], P(('grp', 'req')), parts along dimension 0, may hold values from 1 to 32
- cache_len: int32 [1024], P(('grp', 'req')), parts along dimension 0, may hold values from 0 to 32
- series_perm: int32 [1024], P(('grp', 'req')), parts along dimension 0, may hold values from 0 to 511, each once
- ff_gain: float32 [1280], replicated, may hold values from 0.5 to 1.5
- w_up: bfloat16 [1280, 1280], replicated, may hold values from -0.15625 to 0.15625
- w_down: bfloat16 [1280, 1280], replicated, may hold values from -0.15625 to 0.15625
Outputs:
- packed_out: bfloat16 [32768, 1280], P(('grp', 'req')), parts along dimension 0
The draws below stay inside these ranges and needn't reach their ends.
There are 2 independent parts, one for each index of `grp`. The reference program is written for one: setup_inputs(seed, part) draws one part's arguments, and reference() takes and returns one part's arrays. A program takes and returns all parts, laid end to end along the dimension named above; an argument that names none is the same for every part. Nothing has to cross between parts.
Inputs may be any that keep to these rules, and one draw needn't show every extreme that they name: `series_perm`: each series id appears once.
All inputs are finite; a program needn't handle non-finite values.
Results may differ from the reference program's by a relative error of at most 0.0055.
Values may be sent and summed in bfloat16 or wider, within the bound.
No kernel may reach another device: no remote copies, remote signals or barrier semaphores. Data moves between devices by JAX's collectives and lax.ppermute only.
A program may use at most 64 MiB of HBM per device.

```python
import jax
import jax.numpy as jnp
from jax import lax

D = 1280
H = 16
HD = 80
FF = 1280
S_DEV = 4
SPAN = 32
CACHE = 32
SERIES = 512
TOKCAP = 16384
N_REQ = 128


def draw_new_qkv(key, part):
    base_key = jax.random.fold_in(key, 1)
    base = jnp.clip(jax.random.normal(base_key, (SERIES, SPAN, 3 * D), jnp.float32), -4.5, 4.5)
    return base.astype(jnp.bfloat16)


def draw_cache_kv(key, part):
    base_key = jax.random.fold_in(key, 2)
    base = jnp.clip(jax.random.normal(base_key, (SERIES, CACHE, 2 * D), jnp.float32), -4.5, 4.5)
    return base.astype(jnp.bfloat16)


def draw_span_len(key, part):
    key_len, key_pick = jax.random.split(jax.random.fold_in(key, 3))
    lengths = jax.random.randint(key_len, (SERIES,), 1, SPAN + 1)
    picked = jax.random.randint(key_pick, (), 0, SERIES)
    lengths = lengths.at[picked].set(SPAN)
    lengths = lengths.at[(picked + 1) % SERIES].set(1)
    return lengths.astype(jnp.int32)


def draw_cache_len(key, part):
    key_len, key_pick = jax.random.split(jax.random.fold_in(key, 4))
    lengths = jax.random.randint(key_len, (SERIES,), 0, CACHE + 1)
    picked = jax.random.randint(key_pick, (), 0, SERIES)
    lengths = lengths.at[picked].set(CACHE)
    lengths = lengths.at[(picked + 1) % SERIES].set(0)
    return lengths.astype(jnp.int32)


def block_scale(key, dims, cuts, smallest, high):
    loudness = 1.0
    for axis_at, shards_of in cuts:
        steps = jax.random.uniform(jax.random.fold_in(jax.random.fold_in(key, 6), axis_at), (shards_of,), jnp.float32, smallest / len(cuts), high / len(cuts))
        loudness = loudness * jnp.repeat(jnp.exp(steps), dims[axis_at] // shards_of).reshape((-1,) + (1,) * (len(dims) - 1 - axis_at))
    return loudness


def normal_values(stream_key, extent, spread, limit, cuts=(), kind=jnp.bfloat16):
    entries = spread * jax.random.normal(stream_key, extent, jnp.float32)
    if cuts:
        entries = entries * block_scale(stream_key, extent, cuts, -0.22, 0.18)
    return jnp.clip(entries, -limit, limit).astype(kind)


def setup_inputs(seed: int = 0, part: int = 0) -> dict:
    splits = jax.random.split(jax.random.key(seed), 10)
    part_keys = jax.random.split(jax.random.fold_in(splits[9], part), 10)
    return {
        "new_qkv": draw_new_qkv(jax.random.fold_in(jax.random.fold_in(splits[9], part), 71), part),
        "cache_kv": draw_cache_kv(jax.random.fold_in(jax.random.fold_in(splits[9], part), 71), part),
        "resid": normal_values(part_keys[2], (SERIES, SPAN, D), 1.0, 6.0, ((0, 128),)),
        "span_len": draw_span_len(jax.random.fold_in(jax.random.fold_in(splits[9], part), 71), part),
        "cache_len": draw_cache_len(jax.random.fold_in(jax.random.fold_in(splits[9], part), 71), part),
        "series_perm": jax.random.permutation(part_keys[5], SERIES).astype(jnp.int32),
        "ff_gain": jnp.clip(jax.random.uniform(splits[6], (D,), jnp.float32, 0.5, 1.5), 0.5, 1.5),
        "w_up": normal_values(splits[7], (D, FF), D ** -0.5, 0.15625),
        "w_down": normal_values(splits[8], (FF, D), FF ** -0.5, 0.15625),
    }


def attend_series(series_args):
    new_rows, cached, new_count, cached_count = series_args
    queries = new_rows[:, :D].astype(jnp.float32).reshape(SPAN, H, HD)
    key_rows = jnp.concatenate([cached[:, :D], new_rows[:, D:2 * D]], axis=0).astype(jnp.float32).reshape(CACHE + SPAN, H, HD)
    value_rows = jnp.concatenate([cached[:, D:], new_rows[:, 2 * D:]], axis=0).astype(jnp.float32).reshape(CACHE + SPAN, H, HD)
    scores = jnp.einsum('thd,khd->htk', queries, key_rows) * HD ** (-0.5)
    key_pos = jnp.arange(CACHE + SPAN, dtype=jnp.int32)[None, :]
    row_pos = jnp.arange(SPAN, dtype=jnp.int32)[:, None]
    visible = jnp.where(key_pos < CACHE, key_pos < cached_count, key_pos - CACHE <= row_pos)
    scores = jnp.where(visible[None], scores, -1e+30)
    row_top = lax.optimization_barrier(jnp.max(scores, axis=-1, keepdims=True))
    expo_terms = jnp.exp(scores - row_top)
    weights = expo_terms / lax.optimization_barrier(jnp.sum(expo_terms, axis=-1, keepdims=True))
    weights = lax.optimization_barrier(weights.astype(jnp.bfloat16)).astype(jnp.float32)
    attended = jnp.einsum('htk,khd->thd', weights, value_rows)
    return attended.reshape(SPAN, D)

def feed_forward(hidden, ff_gain, w_up, w_down):
    wide_rows = hidden.astype(jnp.float32)
    normed = (wide_rows * lax.rsqrt(lax.optimization_barrier(jnp.mean(wide_rows * wide_rows, axis=-1, keepdims=True)) + 1e-06) * ff_gain).astype(jnp.bfloat16)
    activated = jax.nn.silu(jnp.dot(normed, w_up, preferred_element_type=jnp.float32)).astype(jnp.bfloat16)
    return (wide_rows + jnp.dot(activated, w_down, preferred_element_type=jnp.float32)).astype(jnp.bfloat16)

def reference(new_qkv, cache_kv, resid, span_len, cache_len, series_perm, ff_gain, w_up, w_down):
    attended = lax.map(attend_series, (new_qkv, cache_kv, span_len, cache_len))
    hidden = (resid.astype(jnp.float32) + attended).astype(jnp.bfloat16)
    count_by_id = jnp.zeros((SERIES,), jnp.int32).at[series_perm].set(span_len)
    start_by_id = (jnp.cumsum(count_by_id) - count_by_id).astype(jnp.int32)
    slot_index = jnp.arange(SPAN, dtype=jnp.int32)
    packed_index = (start_by_id[series_perm][:, None] + slot_index[None, :]).astype(jnp.int32)
    live_slot = slot_index[None, :] < span_len[:, None]
    out_row = packed_index % N_REQ * (S_DEV * SPAN) + packed_index // N_REQ
    out_row = jnp.where(live_slot, out_row, TOKCAP).astype(jnp.int32).reshape(-1)
    layer_out = feed_forward(hidden.reshape(SERIES * SPAN, D), ff_gain, w_up, w_down)
    packed_out = jnp.zeros((TOKCAP, D), jnp.bfloat16).at[out_row].set(layer_out, mode='drop')
    return packed_out
```

```python
import jax
import jax.numpy as jnp
from jax import lax
from jax.experimental import pallas as pl
from jax.experimental.pallas import tpu as pltpu
from jax.sharding import PartitionSpec as P

H = 16


def block_kernel(cache_len_ref, qkv_ref, cache_ref, resid_ref, gain_ref, up_ref, down_ref, out_ref):
    s = pl.program_id(0)
    span_slots = qkv_ref.shape[1]
    cache_slots = cache_ref.shape[1]
    width = resid_ref.shape[2]
    head_size = width // H
    q = qkv_ref[0, :, 0:width]
    k_new = qkv_ref[0, :, width : 2 * width]
    v_new = qkv_ref[0, :, 2 * width : 3 * width]
    k_old = cache_ref[0, :, 0:width]
    v_old = cache_ref[0, :, width : 2 * width]
    col_head = lax.broadcasted_iota(jnp.int32, (H, 1, width), 2) // head_size
    head_id = lax.broadcasted_iota(jnp.int32, (H, 1, width), 0)
    head_mask = col_head == head_id
    q_heads = jnp.where(head_mask, q[None], jnp.zeros((), q.dtype)).reshape(H * span_slots, width)
    dims = (((1,), (1,)), ((), ()))
    scale = head_size ** (-0.5)
    s_old = lax.dot_general(q_heads, k_old, dims, preferred_element_type=jnp.float32) * scale
    s_new = lax.dot_general(q_heads, k_new, dims, preferred_element_type=jnp.float32) * scale
    rows = H * span_slots
    row_t = lax.broadcasted_iota(jnp.int32, (rows, span_slots), 0) % span_slots
    key_new = lax.broadcasted_iota(jnp.int32, (rows, span_slots), 1)
    key_old = lax.broadcasted_iota(jnp.int32, (rows, cache_slots), 1)
    s_old = jnp.where(key_old < cache_len_ref[s], s_old, -1e30)
    s_new = jnp.where(key_new <= row_t, s_new, -1e30)
    top = jnp.maximum(jnp.max(s_old, axis=1, keepdims=True), jnp.max(s_new, axis=1, keepdims=True))
    e_old = jnp.exp(s_old - top)
    e_new = jnp.exp(s_new - top)
    denom = jnp.sum(e_old, axis=1, keepdims=True) + jnp.sum(e_new, axis=1, keepdims=True)
    w_old = (e_old / denom).astype(jnp.bfloat16)
    w_new = (e_new / denom).astype(jnp.bfloat16)
    mixed = jnp.dot(w_old, v_old, preferred_element_type=jnp.float32) + jnp.dot(
        w_new, v_new, preferred_element_type=jnp.float32
    )
    mixed = mixed.reshape(H, span_slots, width)
    attended = jnp.sum(jnp.where(head_mask, mixed, 0.0), axis=0)
    hidden = (resid_ref[0].astype(jnp.float32) + attended).astype(jnp.bfloat16)
    wide_rows = hidden.astype(jnp.float32)
    normed = (
        wide_rows
        * lax.rsqrt(jnp.mean(wide_rows * wide_rows, axis=-1, keepdims=True) + 1e-06)
        * gain_ref[...]
    ).astype(jnp.bfloat16)
    activated = jax.nn.silu(
        jnp.dot(normed, up_ref[...], preferred_element_type=jnp.float32)
    ).astype(jnp.bfloat16)
    out_ref[0] = (
        wide_rows + jnp.dot(activated, down_ref[...], preferred_element_type=jnp.float32)
    ).astype(out_ref.dtype)


def layer_block(new_qkv, cache_kv, resid, cache_len, ff_gain, w_up, w_down):
    series_here, span_slots, triple = new_qkv.shape
    cache_slots, pair = cache_kv.shape[1], cache_kv.shape[2]
    width = resid.shape[2]
    grid_spec = pltpu.PrefetchScalarGridSpec(
        num_scalar_prefetch=1,
        grid=(series_here,),
        in_specs=[
            pl.BlockSpec((1, span_slots, triple), lambda s, cl: (s, 0, 0)),
            pl.BlockSpec((1, cache_slots, pair), lambda s, cl: (s, 0, 0)),
            pl.BlockSpec((1, span_slots, width), lambda s, cl: (s, 0, 0)),
            pl.BlockSpec((1, width), lambda s, cl: (0, 0)),
            pl.BlockSpec(w_up.shape, lambda s, cl: (0, 0)),
            pl.BlockSpec(w_down.shape, lambda s, cl: (0, 0)),
        ],
        out_specs=pl.BlockSpec((1, span_slots, width), lambda s, cl: (s, 0, 0)),
    )
    return pl.pallas_call(
        block_kernel,
        grid_spec=grid_spec,
        out_shape=jax.ShapeDtypeStruct((series_here, span_slots, width), jnp.bfloat16),
        compiler_params=pltpu.CompilerParams(dimension_semantics=("arbitrary",)),
    )(cache_len, new_qkv, cache_kv, resid, ff_gain.reshape(1, width), w_up, w_down)


def local(new_qkv, cache_kv, resid, span_len, cache_len, series_perm, ff_gain, w_up, w_down):
    group_size = lax.axis_size("req")
    me = lax.axis_index("req")
    series_here, span_slots, triple = new_qkv.shape
    width = resid.shape[2]
    gathered = lax.all_gather(jnp.stack([span_len, series_perm]), "req", axis=1, tiled=True)
    all_len, all_perm = gathered[0], gathered[1]
    series_total = all_len.shape[0]
    earlier = all_perm[None, :] < all_perm[:, None]
    all_start = jnp.sum(jnp.where(earlier, all_len[None, :], 0), axis=1)

    layer_out = layer_block(new_qkv, cache_kv, resid, cache_len, ff_gain, w_up, w_down)

    my_start = lax.dynamic_slice(all_start, (me * series_here,), (series_here,))
    target = jnp.arange(group_size, dtype=jnp.int32)[None, :, None]
    slot = jnp.arange(span_slots, dtype=jnp.int32)[None, None, :]
    my_offset = (target - my_start[:, None, None]) % group_size
    pick = (my_offset == slot) & (slot < span_len[:, None, None])
    pick = pick.astype(jnp.bfloat16)
    placed = jnp.concatenate(
        [
            jnp.dot(pick[i], layer_out[i], preferred_element_type=jnp.float32).astype(jnp.bfloat16)
            for i in range(series_here)
        ],
        axis=1,
    )
    arrived = lax.all_to_all(placed, "req", split_axis=0, concat_axis=0, tiled=True)

    src_start = all_start.reshape(group_size, series_here)
    src_len = all_len.reshape(group_size, series_here)
    src_t = (me - src_start) % group_size
    src_row = (src_start + src_t) // group_size
    src_row = jnp.where(src_t < src_len, src_row, -1)
    rows_here = series_here * span_slots
    out_row = jnp.arange(rows_here, dtype=jnp.int32)[:, None]
    result = jnp.zeros((rows_here, width), jnp.float32)
    for i in range(series_here):
        gather_i = (src_row[None, :, i] == out_row).astype(jnp.bfloat16)
        result = result + jnp.dot(
            gather_i, arrived[:, i * width : (i + 1) * width], preferred_element_type=jnp.float32
        )
    return result.astype(jnp.bfloat16)


def solution(mesh):
    in_specs = (
        P(("grp", "req"), None, None),
        P(("grp", "req"), None, None),
        P(("grp", "req"), None, None),
        P(("grp", "req")),
        P(("grp", "req")),
        P(("grp", "req")),
        P(),
        P(),
        P(),
    )
    out_specs = P(("grp", "req"), None)
    return jax.shard_map(local, mesh=mesh, in_specs=in_specs, out_specs=out_specs, check_vma=False)
```

```python
import jax
import jax.numpy as jnp
from jax import lax
from jax.experimental import pallas as pl
from jax.experimental.pallas import tpu as pltpu
from jax.sharding import PartitionSpec as P

H = 16


def block_kernel(cache_len_ref, qkv_ref, cache_ref, resid_ref, gain_ref, up_ref, down_ref, out_ref):
    s = pl.program_id(0)
    span_slots = qkv_ref.shape[1]
    cache_slots = cache_ref.shape[1]
    width = resid_ref.shape[2]
    head_size = width // H
    q = qkv_ref[0, :, 0:width]
    k_new = qkv_ref[0, :, width : 2 * width]
    v_new = qkv_ref[0, :, 2 * width : 3 * width]
    k_old = cache_ref[0, :, 0:width]
    v_old = cache_ref[0, :, width : 2 * width]
    col_head = lax.broadcasted_iota(jnp.int32, (H, 1, width), 2) // head_size
    head_id = lax.broadcasted_iota(jnp.int32, (H, 1, width), 0)
    head_mask = col_head == head_id
    q_heads = jnp.where(head_mask, q[None], jnp.zeros((), q.dtype)).reshape(H * span_slots, width)
    dims = (((1,), (1,)), ((), ()))
    scale = head_size ** (-0.5)
    s_old = lax.dot_general(q_heads, k_old, dims, preferred_element_type=jnp.float32) * scale
    s_new = lax.dot_general(q_heads, k_new, dims, preferred_element_type=jnp.float32) * scale
    rows = H * span_slots
    row_t = lax.broadcasted_iota(jnp.int32, (rows, span_slots), 0) % span_slots
    key_new = lax.broadcasted_iota(jnp.int32, (rows, span_slots), 1)
    key_old = lax.broadcasted_iota(jnp.int32, (rows, cache_slots), 1)
    s_old = jnp.where(key_old < cache_len_ref[s], s_old, -1e30)
    s_new = jnp.where(key_new <= row_t, s_new, -1e30)
    top = jnp.maximum(jnp.max(s_old, axis=1, keepdims=True), jnp.max(s_new, axis=1, keepdims=True))
    e_old = jnp.exp(s_old - top)
    e_new = jnp.exp(s_new - top)
    denom = jnp.sum(e_old, axis=1, keepdims=True) + jnp.sum(e_new, axis=1, keepdims=True)
    w_old = (e_old / denom).astype(jnp.bfloat16)
    w_new = (e_new / denom).astype(jnp.bfloat16)
    mixed = jnp.dot(w_old, v_old, preferred_element_type=jnp.float32) + jnp.dot(
        w_new, v_new, preferred_element_type=jnp.float32
    )
    mixed = mixed.reshape(H, span_slots, width)
    attended = jnp.sum(jnp.where(head_mask, mixed, 0.0), axis=0)
    hidden = (resid_ref[0].astype(jnp.float32) + attended).astype(jnp.bfloat16)
    wide_rows = hidden.astype(jnp.float32)
    normed = (
        wide_rows
        * lax.rsqrt(jnp.mean(wide_rows * wide_rows, axis=-1, keepdims=True) + 1e-06)
        * gain_ref[...]
    ).astype(jnp.bfloat16)
    activated = jax.nn.silu(
        jnp.dot(normed, up_ref[...], preferred_element_type=jnp.float32)
    ).astype(jnp.bfloat16)
    out_ref[0] = (
        wide_rows + jnp.dot(activated, down_ref[...], preferred_element_type=jnp.float32)
    ).astype(out_ref.dtype)


def layer_block(new_qkv, cache_kv, resid, cache_len, ff_gain, w_up, w_down):
    series_here, span_slots, triple = new_qkv.shape
    cache_slots, pair = cache_kv.shape[1], cache_kv.shape[2]
    width = resid.shape[2]
    grid_spec = pltpu.PrefetchScalarGridSpec(
        num_scalar_prefetch=1,
        grid=(series_here,),
        in_specs=[
            pl.BlockSpec((1, span_slots, triple), lambda s, cl: (s, 0, 0)),
            pl.BlockSpec((1, cache_slots, pair), lambda s, cl: (s, 0, 0)),
            pl.BlockSpec((1, span_slots, width), lambda s, cl: (s, 0, 0)),
            pl.BlockSpec((1, width), lambda s, cl: (0, 0)),
            pl.BlockSpec(w_up.shape, lambda s, cl: (0, 0)),
            pl.BlockSpec(w_down.shape, lambda s, cl: (0, 0)),
        ],
        out_specs=pl.BlockSpec((1, span_slots, width), lambda s, cl: (s, 0, 0)),
    )
    return pl.pallas_call(
        block_kernel,
        grid_spec=grid_spec,
        out_shape=jax.ShapeDtypeStruct((series_here, span_slots, width), jnp.bfloat16),
        compiler_params=pltpu.CompilerParams(dimension_semantics=("arbitrary",)),
    )(cache_len, new_qkv, cache_kv, resid, ff_gain.reshape(1, width), w_up, w_down)


def local(new_qkv, cache_kv, resid, span_len, cache_len, series_perm, ff_gain, w_up, w_down):
    group_size = lax.axis_size("req")
    me = lax.axis_index("req")
    series_here, span_slots, triple = new_qkv.shape
    width = resid.shape[2]
    info = jnp.concatenate([span_len, series_perm])
    gathered = lax.all_to_all(
        jnp.broadcast_to(info[None], (group_size, info.shape[0])), "req", 0, 0, tiled=True
    )
    all_len = gathered[:, :series_here].reshape(-1)
    all_perm = gathered[:, series_here:].reshape(-1)
    series_total = all_len.shape[0]
    earlier = all_perm[None, :] < all_perm[:, None]
    all_start = jnp.sum(jnp.where(earlier, all_len[None, :], 0), axis=1)

    layer_out = layer_block(new_qkv, cache_kv, resid, cache_len, ff_gain, w_up, w_down)

    my_start = lax.dynamic_slice(all_start, (me * series_here,), (series_here,))
    target = jnp.arange(group_size, dtype=jnp.int32)[None, :, None]
    slot = jnp.arange(span_slots, dtype=jnp.int32)[None, None, :]
    my_offset = (target - my_start[:, None, None]) % group_size
    pick = (my_offset == slot) & (slot < span_len[:, None, None])
    pick = pick.astype(jnp.bfloat16)

    src_start = all_start.reshape(group_size, series_here)
    src_len = all_len.reshape(group_size, series_here)
    src_t = (me - src_start) % group_size
    src_row = (src_start + src_t) // group_size
    src_row = jnp.where(src_t < src_len, src_row, -1)
    rows_here = series_here * span_slots
    out_row = jnp.arange(rows_here, dtype=jnp.int32)[:, None]
    result = jnp.zeros((rows_here, width), jnp.float32)
    for i in range(series_here):
        placed = jnp.dot(pick[i], layer_out[i], preferred_element_type=jnp.float32).astype(jnp.bfloat16)
        arrived = lax.all_to_all(placed, "req", 0, 0, tiled=True)
        gather_i = (src_row[None, :, i] == out_row).astype(jnp.bfloat16)
        result = result + jnp.dot(gather_i, arrived, preferred_element_type=jnp.float32)
    return result.astype(jnp.bfloat16)


def solution(mesh):
    in_specs = (
        P(("grp", "req"), None, None),
        P(("grp", "req"), None, None),
        P(("grp", "req"), None, None),
        P(("grp", "req")),
        P(("grp", "req")),
        P(("grp", "req")),
        P(),
        P(),
        P(),
    )
    out_specs = P(("grp", "req"), None)
    return jax.shard_map(local, mesh=mesh, in_specs=in_specs, out_specs=out_specs, check_vma=False)
```

```python
import jax
import jax.numpy as jnp
from jax import lax
from jax.experimental import pallas as pl
from jax.experimental.pallas import tpu as pltpu
from jax.sharding import PartitionSpec as P

H = 16


def block_kernel(cache_len_ref, qkv_ref, cache_ref, resid_ref, gain_ref, up_ref, down_ref, out_ref):
    s = pl.program_id(0)
    span_slots = qkv_ref.shape[1]
    cache_slots = cache_ref.shape[1]
    width = resid_ref.shape[2]
    head_size = width // H
    q = qkv_ref[0, :, 0:width]
    k_new = qkv_ref[0, :, width : 2 * width]
    v_new = qkv_ref[0, :, 2 * width : 3 * width]
    k_old = cache_ref[0, :, 0:width]
    v_old = cache_ref[0, :, width : 2 * width]
    col_head = lax.broadcasted_iota(jnp.int32, (H, 1, width), 2) // head_size
    head_id = lax.broadcasted_iota(jnp.int32, (H, 1, width), 0)
    head_mask = col_head == head_id
    q_heads = jnp.where(head_mask, q[None], jnp.zeros((), q.dtype)).reshape(H * span_slots, width)
    dims = (((1,), (1,)), ((), ()))
    scale = head_size ** (-0.5)
    s_old = lax.dot_general(q_heads, k_old, dims, preferred_element_type=jnp.float32) * scale
    s_new = lax.dot_general(q_heads, k_new, dims, preferred_element_type=jnp.float32) * scale
    rows = H * span_slots
    row_t = lax.broadcasted_iota(jnp.int32, (rows, span_slots), 0) % span_slots
    key_new = lax.broadcasted_iota(jnp.int32, (rows, span_slots), 1)
    key_old = lax.broadcasted_iota(jnp.int32, (rows, cache_slots), 1)
    s_old = jnp.where(key_old < cache_len_ref[s], s_old, -1e30)
    s_new = jnp.where(key_new <= row_t, s_new, -1e30)
    top = jnp.maximum(jnp.max(s_old, axis=1, keepdims=True), jnp.max(s_new, axis=1, keepdims=True))
    e_old = jnp.exp(s_old - top)
    e_new = jnp.exp(s_new - top)
    denom = jnp.sum(e_old, axis=1, keepdims=True) + jnp.sum(e_new, axis=1, keepdims=True)
    w_old = (e_old / denom).astype(jnp.bfloat16)
    w_new = (e_new / denom).astype(jnp.bfloat16)
    mixed = jnp.dot(w_old, v_old, preferred_element_type=jnp.float32) + jnp.dot(
        w_new, v_new, preferred_element_type=jnp.float32
    )
    mixed = mixed.reshape(H, span_slots, width)
    attended = jnp.sum(jnp.where(head_mask, mixed, 0.0), axis=0)
    hidden = (resid_ref[0].astype(jnp.float32) + attended).astype(jnp.bfloat16)
    wide_rows = hidden.astype(jnp.float32)
    normed = (
        wide_rows
        * lax.rsqrt(jnp.mean(wide_rows * wide_rows, axis=-1, keepdims=True) + 1e-06)
        * gain_ref[...]
    ).astype(jnp.bfloat16)
    activated = jax.nn.silu(
        jnp.dot(normed, up_ref[...], preferred_element_type=jnp.float32)
    ).astype(jnp.bfloat16)
    out_ref[0] = (
        wide_rows + jnp.dot(activated, down_ref[...], preferred_element_type=jnp.float32)
    ).astype(out_ref.dtype)


def layer_block(new_qkv, cache_kv, resid, cache_len, ff_gain, w_up, w_down):
    series_here, span_slots, triple = new_qkv.shape
    cache_slots, pair = cache_kv.shape[1], cache_kv.shape[2]
    width = resid.shape[2]
    grid_spec = pltpu.PrefetchScalarGridSpec(
        num_scalar_prefetch=1,
        grid=(series_here,),
        in_specs=[
            pl.BlockSpec((1, span_slots, triple), lambda s, cl: (s, 0, 0)),
            pl.BlockSpec((1, cache_slots, pair), lambda s, cl: (s, 0, 0)),
            pl.BlockSpec((1, span_slots, width), lambda s, cl: (s, 0, 0)),
            pl.BlockSpec((1, width), lambda s, cl: (0, 0)),
            pl.BlockSpec(w_up.shape, lambda s, cl: (0, 0)),
            pl.BlockSpec(w_down.shape, lambda s, cl: (0, 0)),
        ],
        out_specs=pl.BlockSpec((1, span_slots, width), lambda s, cl: (s, 0, 0)),
    )
    return pl.pallas_call(
        block_kernel,
        grid_spec=grid_spec,
        out_shape=jax.ShapeDtypeStruct((series_here, span_slots, width), jnp.bfloat16),
        compiler_params=pltpu.CompilerParams(dimension_semantics=("arbitrary",)),
    )(cache_len, new_qkv, cache_kv, resid, ff_gain.reshape(1, width), w_up, w_down)


def local(new_qkv, cache_kv, resid, span_len, cache_len, series_perm, ff_gain, w_up, w_down):
    group_size = lax.axis_size("req")
    me = lax.axis_index("req")
    series_here, span_slots, triple = new_qkv.shape
    width = resid.shape[2]
    info = jnp.concatenate([span_len, series_perm])
    gathered = lax.all_to_all(
        jnp.broadcast_to(info[None], (group_size, info.shape[0])), "req", 0, 0, tiled=True
    )
    all_len = gathered[:, :series_here].reshape(-1)
    all_perm = gathered[:, series_here:].reshape(-1)
    series_total = all_len.shape[0]
    earlier = all_perm[None, :] < all_perm[:, None]
    all_start = jnp.sum(jnp.where(earlier, all_len[None, :], 0), axis=1)

    layer_out = layer_block(new_qkv, cache_kv, resid, cache_len, ff_gain, w_up, w_down)

    my_start = lax.dynamic_slice(all_start, (me * series_here,), (series_here,))
    target = jnp.arange(group_size, dtype=jnp.int32)[None, :, None]
    slot = jnp.arange(span_slots, dtype=jnp.int32)[None, None, :]
    my_offset = (target - my_start[:, None, None]) % group_size
    pick = (my_offset == slot) & (slot < span_len[:, None, None])
    pick = pick.astype(jnp.bfloat16)

    src_start = all_start.reshape(group_size, series_here)
    src_len = all_len.reshape(group_size, series_here)
    src_t = (me - src_start) % group_size
    src_row = (src_start + src_t) // group_size
    src_row = jnp.where(src_t < src_len, src_row, -1)
    rows_here = series_here * span_slots
    out_row = jnp.arange(rows_here, dtype=jnp.int32)[:, None]
    placed = jnp.einsum(
        "idt,itc->dic", pick, layer_out, preferred_element_type=jnp.float32
    ).astype(jnp.bfloat16)
    placed = placed.reshape(group_size * series_here, width)
    arrived = lax.all_to_all(placed, "req", 0, 0, tiled=True)
    gather = (src_row.reshape(1, -1) == out_row).astype(jnp.bfloat16)
    result = jnp.dot(gather, arrived, preferred_element_type=jnp.float32)
    return result.astype(jnp.bfloat16)


def solution(mesh):
    in_specs = (
        P(("grp", "req"), None, None),
        P(("grp", "req"), None, None),
        P(("grp", "req"), None, None),
        P(("grp", "req")),
        P(("grp", "req")),
        P(("grp", "req")),
        P(),
        P(),
        P(),
    )
    out_specs = P(("grp", "req"), None)
    return jax.shard_map(local, mesh=mesh, in_specs=in_specs, out_specs=out_specs, check_vma=False)
```

```python
import jax
import jax.numpy as jnp
from jax import lax
from jax.experimental import pallas as pl
from jax.experimental.pallas import tpu as pltpu
from jax.sharding import PartitionSpec as P

H = 16


def block_kernel(cache_len_ref, qkv_ref, cache_ref, resid_ref, gain_ref, up_ref, down_ref, pick_ref, out_ref, hid_ref):
    series_here, span_slots = qkv_ref.shape[0], qkv_ref.shape[1]
    cache_slots = cache_ref.shape[1]
    width = resid_ref.shape[2]
    head_size = width // H
    col_head = lax.broadcasted_iota(jnp.int32, (H, 1, width), 2) // head_size
    head_id = lax.broadcasted_iota(jnp.int32, (H, 1, width), 0)
    head_mask = col_head == head_id
    dims = (((1,), (1,)), ((), ()))
    scale = head_size ** (-0.5)
    rows = H * span_slots
    row_t = lax.broadcasted_iota(jnp.int32, (rows, span_slots), 0) % span_slots
    key_new = lax.broadcasted_iota(jnp.int32, (rows, span_slots), 1)
    key_old = lax.broadcasted_iota(jnp.int32, (rows, cache_slots), 1)
    for i in range(series_here):
        q = qkv_ref[i, :, 0:width]
        k_new = qkv_ref[i, :, width : 2 * width]
        v_new = qkv_ref[i, :, 2 * width : 3 * width]
        k_old = cache_ref[i, :, 0:width]
        v_old = cache_ref[i, :, width : 2 * width]
        q_heads = jnp.where(head_mask, q[None], jnp.zeros((), q.dtype)).reshape(rows, width)
        s_old = lax.dot_general(q_heads, k_old, dims, preferred_element_type=jnp.float32) * scale
        s_new = lax.dot_general(q_heads, k_new, dims, preferred_element_type=jnp.float32) * scale
        s_old = jnp.where(key_old < cache_len_ref[i], s_old, -1e30)
        s_new = jnp.where(key_new <= row_t, s_new, -1e30)
        top = jnp.maximum(jnp.max(s_old, axis=1, keepdims=True), jnp.max(s_new, axis=1, keepdims=True))
        e_old = jnp.exp(s_old - top)
        e_new = jnp.exp(s_new - top)
        denom = jnp.sum(e_old, axis=1, keepdims=True) + jnp.sum(e_new, axis=1, keepdims=True)
        w_old = (e_old / denom).astype(jnp.bfloat16)
        w_new = (e_new / denom).astype(jnp.bfloat16)
        mixed = jnp.dot(w_old, v_old, preferred_element_type=jnp.float32) + jnp.dot(
            w_new, v_new, preferred_element_type=jnp.float32
        )
        mixed = mixed.reshape(H, span_slots, width)
        attended = jnp.sum(jnp.where(head_mask, mixed, 0.0), axis=0)
        hid_ref[i * span_slots : (i + 1) * span_slots, :] = (
            resid_ref[i].astype(jnp.float32) + attended
        ).astype(hid_ref.dtype)
    wide_rows = hid_ref[...].astype(jnp.float32)
    normed = (
        wide_rows
        * lax.rsqrt(jnp.mean(wide_rows * wide_rows, axis=-1, keepdims=True) + 1e-06)
        * gain_ref[...]
    ).astype(jnp.bfloat16)
    activated = jax.nn.silu(
        jnp.dot(normed, up_ref[...], preferred_element_type=jnp.float32)
    ).astype(jnp.bfloat16)
    layer_out = (
        wide_rows + jnp.dot(activated, down_ref[...], preferred_element_type=jnp.float32)
    ).astype(jnp.bfloat16)
    out_ref[...] = jnp.dot(pick_ref[...], layer_out, preferred_element_type=jnp.float32).astype(
        out_ref.dtype
    )


def layer_block(new_qkv, cache_kv, resid, cache_len, ff_gain, w_up, w_down, pick):
    series_here, span_slots, triple = new_qkv.shape
    width = resid.shape[2]
    vmem = pltpu.MemorySpace.VMEM if hasattr(pltpu, "MemorySpace") else pltpu.VMEM
    full = pl.BlockSpec(memory_space=vmem)
    return pl.pallas_call(
        block_kernel,
        in_specs=[pl.BlockSpec(memory_space=pltpu.SMEM)] + [full] * 7,
        out_specs=full,
        out_shape=jax.ShapeDtypeStruct((pick.shape[0], width), jnp.bfloat16),
        scratch_shapes=[pltpu.VMEM((series_here * span_slots, width), jnp.bfloat16)],
    )(cache_len, new_qkv, cache_kv, resid, ff_gain.reshape(1, width), w_up, w_down, pick)


def local(new_qkv, cache_kv, resid, span_len, cache_len, series_perm, ff_gain, w_up, w_down):
    group_size = lax.axis_size("req")
    me = lax.axis_index("req")
    series_here, span_slots, triple = new_qkv.shape
    width = resid.shape[2]
    info = jnp.concatenate([span_len, series_perm])
    gathered = lax.all_to_all(
        jnp.broadcast_to(info[None], (group_size, info.shape[0])), "req", 0, 0, tiled=True
    )
    all_len = gathered[:, :series_here].reshape(-1)
    all_perm = gathered[:, series_here:].reshape(-1)
    series_total = all_len.shape[0]
    earlier = all_perm[None, :] < all_perm[:, None]
    all_start = jnp.sum(jnp.where(earlier, all_len[None, :], 0), axis=1)


    my_start = lax.dynamic_slice(all_start, (me * series_here,), (series_here,))
    target = jnp.arange(group_size, dtype=jnp.int32)[None, :, None]
    slot = jnp.arange(span_slots, dtype=jnp.int32)[None, None, :]
    my_offset = (target - my_start[:, None, None]) % group_size
    pick = (my_offset == slot) & (slot < span_len[:, None, None])
    same = jnp.arange(series_here)[:, None] == jnp.arange(series_here)[None, :]
    pick = pick.transpose(1, 0, 2)[:, :, None, :] & same[None, :, :, None]
    pick = pick.reshape(group_size * series_here, series_here * span_slots).astype(jnp.bfloat16)

    src_start = all_start.reshape(group_size, series_here)
    src_len = all_len.reshape(group_size, series_here)
    src_t = (me - src_start) % group_size
    src_row = (src_start + src_t) // group_size
    src_row = jnp.where(src_t < src_len, src_row, -1)
    rows_here = series_here * span_slots
    out_row = jnp.arange(rows_here, dtype=jnp.int32)[:, None]
    placed = layer_block(new_qkv, cache_kv, resid, cache_len, ff_gain, w_up, w_down, pick)
    arrived = lax.all_to_all(placed, "req", 0, 0, tiled=True)
    gather = (src_row.reshape(1, -1) == out_row).astype(jnp.bfloat16)
    result = jnp.dot(gather, arrived, preferred_element_type=jnp.float32)
    return result.astype(jnp.bfloat16)


def solution(mesh):
    in_specs = (
        P(("grp", "req"), None, None),
        P(("grp", "req"), None, None),
        P(("grp", "req"), None, None),
        P(("grp", "req")),
        P(("grp", "req")),
        P(("grp", "req")),
        P(),
        P(),
        P(),
    )
    out_specs = P(("grp", "req"), None)
    return jax.shard_map(local, mesh=mesh, in_specs=in_specs, out_specs=out_specs, check_vma=False)
```

```python
import jax
import jax.numpy as jnp
from jax import lax
from jax.experimental import pallas as pl
from jax.experimental.pallas import tpu as pltpu
from jax.sharding import PartitionSpec as P

H = 16


def block_kernel(cache_len_ref, qkv_ref, cache_ref, resid_ref, gain_ref, up_ref, down_ref, out_ref, hid_ref):
    series_here, span_slots = qkv_ref.shape[0], qkv_ref.shape[1]
    cache_slots = cache_ref.shape[1]
    width = resid_ref.shape[2]
    head_size = width // H
    col_head = lax.broadcasted_iota(jnp.int32, (H, 1, width), 2) // head_size
    head_id = lax.broadcasted_iota(jnp.int32, (H, 1, width), 0)
    head_mask = col_head == head_id
    dims = (((1,), (1,)), ((), ()))
    scale = head_size ** (-0.5)
    rows = H * span_slots
    row_t = lax.broadcasted_iota(jnp.int32, (rows, span_slots), 0) % span_slots
    key_new = lax.broadcasted_iota(jnp.int32, (rows, span_slots), 1)
    key_old = lax.broadcasted_iota(jnp.int32, (rows, cache_slots), 1)
    for i in range(series_here):
        q = qkv_ref[i, :, 0:width]
        k_new = qkv_ref[i, :, width : 2 * width]
        v_new = qkv_ref[i, :, 2 * width : 3 * width]
        k_old = cache_ref[i, :, 0:width]
        v_old = cache_ref[i, :, width : 2 * width]
        q_heads = jnp.where(head_mask, q[None], jnp.zeros((), q.dtype)).reshape(rows, width)
        s_old = lax.dot_general(q_heads, k_old, dims, preferred_element_type=jnp.float32) * scale
        s_new = lax.dot_general(q_heads, k_new, dims, preferred_element_type=jnp.float32) * scale
        s_old = jnp.where(key_old < cache_len_ref[i], s_old, -1e30)
        s_new = jnp.where(key_new <= row_t, s_new, -1e30)
        top = jnp.maximum(jnp.max(s_old, axis=1, keepdims=True), jnp.max(s_new, axis=1, keepdims=True))
        e_old = jnp.exp(s_old - top)
        e_new = jnp.exp(s_new - top)
        denom = jnp.sum(e_old, axis=1, keepdims=True) + jnp.sum(e_new, axis=1, keepdims=True)
        w_old = (e_old / denom).astype(jnp.bfloat16)
        w_new = (e_new / denom).astype(jnp.bfloat16)
        mixed = jnp.dot(w_old, v_old, preferred_element_type=jnp.float32) + jnp.dot(
            w_new, v_new, preferred_element_type=jnp.float32
        )
        mixed = mixed.reshape(H, span_slots, width)
        attended = jnp.sum(jnp.where(head_mask, mixed, 0.0), axis=0)
        hid_ref[i * span_slots : (i + 1) * span_slots, :] = (
            resid_ref[i].astype(jnp.float32) + attended
        ).astype(hid_ref.dtype)
    wide_rows = hid_ref[...].astype(jnp.float32)
    normed = (
        wide_rows
        * lax.rsqrt(jnp.mean(wide_rows * wide_rows, axis=-1, keepdims=True) + 1e-06)
        * gain_ref[...]
    ).astype(jnp.bfloat16)
    activated = jax.nn.silu(
        jnp.dot(normed, up_ref[...], preferred_element_type=jnp.float32)
    ).astype(jnp.bfloat16)
    out_ref[...] = (
        wide_rows + jnp.dot(activated, down_ref[...], preferred_element_type=jnp.float32)
    ).astype(out_ref.dtype)


def layer_block(new_qkv, cache_kv, resid, cache_len, ff_gain, w_up, w_down):
    series_here, span_slots, triple = new_qkv.shape
    width = resid.shape[2]
    vmem = pltpu.MemorySpace.VMEM if hasattr(pltpu, "MemorySpace") else pltpu.VMEM
    full = pl.BlockSpec(memory_space=vmem)
    return pl.pallas_call(
        block_kernel,
        in_specs=[pl.BlockSpec(memory_space=pltpu.SMEM)] + [full] * 6,
        out_specs=full,
        out_shape=jax.ShapeDtypeStruct((series_here * span_slots, width), jnp.bfloat16),
        scratch_shapes=[pltpu.VMEM((series_here * span_slots, width), jnp.bfloat16)],
    )(cache_len, new_qkv, cache_kv, resid, ff_gain.reshape(1, width), w_up, w_down)


def local(new_qkv, cache_kv, resid, span_len, cache_len, series_perm, ff_gain, w_up, w_down):
    group_size = lax.axis_size("req")
    me = lax.axis_index("req")
    series_here, span_slots, triple = new_qkv.shape
    width = resid.shape[2]
    layer_out = layer_block(new_qkv, cache_kv, resid, cache_len, ff_gain, w_up, w_down)
    info = jnp.concatenate([span_len, series_perm])
    gathered = lax.all_to_all(
        jnp.broadcast_to(info[None], (group_size, info.shape[0])), "req", 0, 0, tiled=True
    )
    all_len = gathered[:, :series_here].reshape(-1)
    all_perm = gathered[:, series_here:].reshape(-1)
    series_total = all_len.shape[0]
    earlier = all_perm[None, :] < all_perm[:, None]
    all_start = jnp.sum(jnp.where(earlier, all_len[None, :], 0), axis=1)


    my_start = lax.dynamic_slice(all_start, (me * series_here,), (series_here,))
    target = jnp.arange(group_size, dtype=jnp.int32)[None, :, None]
    slot = jnp.arange(span_slots, dtype=jnp.int32)[None, None, :]
    my_offset = (target - my_start[:, None, None]) % group_size
    pick = (my_offset == slot) & (slot < span_len[:, None, None])
    same = jnp.arange(series_here)[:, None] == jnp.arange(series_here)[None, :]
    pick = pick.transpose(1, 0, 2)[:, :, None, :] & same[None, :, :, None]
    pick = pick.reshape(group_size * series_here, series_here * span_slots).astype(jnp.bfloat16)

    src_start = all_start.reshape(group_size, series_here)
    src_len = all_len.reshape(group_size, series_here)
    src_t = (me - src_start) % group_size
    src_row = (src_start + src_t) // group_size
    src_row = jnp.where(src_t < src_len, src_row, -1)
    rows_here = series_here * span_slots
    out_row = jnp.arange(rows_here, dtype=jnp.int32)[:, None]
    placed = lax.dot_general(
        pick.reshape(group_size, series_here, -1),
        layer_out,
        (((2,), (0,)), ((), ())),
        preferred_element_type=jnp.float32,
    ).astype(jnp.bfloat16)
    arrived = lax.all_to_all(placed, "req", 0, 0, tiled=True)
    gather = (src_row.reshape(1, -1) == out_row).astype(jnp.bfloat16)
    result = jnp.dot(gather, arrived.reshape(-1, width), preferred_element_type=jnp.float32)
    return result.astype(jnp.bfloat16)


def solution(mesh):
    in_specs = (
        P(("grp", "req"), None, None),
        P(("grp", "req"), None, None),
        P(("grp", "req"), None, None),
        P(("grp", "req")),
        P(("grp", "req")),
        P(("grp", "req")),
        P(),
        P(),
        P(),
    )
    out_specs = P(("grp", "req"), None)
    return jax.shard_map(local, mesh=mesh, in_specs=in_specs, out_specs=out_specs, check_vma=False)
```

```python
import jax
import jax.numpy as jnp
from jax import lax
from jax.experimental import pallas as pl
from jax.experimental.pallas import tpu as pltpu
from jax.sharding import PartitionSpec as P

H = 16


def block_kernel(cache_len_ref, qkv_ref, cache_ref, resid_ref, gain_ref, up_ref, down_ref, out_ref, hid_ref):
    series_here, span_slots = qkv_ref.shape[0], qkv_ref.shape[1]
    cache_slots = cache_ref.shape[1]
    width = resid_ref.shape[2]
    head_size = width // H
    col_head = lax.broadcasted_iota(jnp.int32, (H, 1, width), 2) // head_size
    head_id = lax.broadcasted_iota(jnp.int32, (H, 1, width), 0)
    head_mask = col_head == head_id
    dims = (((1,), (1,)), ((), ()))
    scale = head_size ** (-0.5)
    rows = H * span_slots
    row_t = lax.broadcasted_iota(jnp.int32, (rows, span_slots), 0) % span_slots
    key_new = lax.broadcasted_iota(jnp.int32, (rows, span_slots), 1)
    key_old = lax.broadcasted_iota(jnp.int32, (rows, cache_slots), 1)
    for i in range(series_here):
        q = qkv_ref[i, :, 0:width]
        k_new = qkv_ref[i, :, width : 2 * width]
        v_new = qkv_ref[i, :, 2 * width : 3 * width]
        k_old = cache_ref[i, :, 0:width]
        v_old = cache_ref[i, :, width : 2 * width]
        q_heads = jnp.where(head_mask, q[None], jnp.zeros((), q.dtype)).reshape(rows, width)
        s_old = lax.dot_general(q_heads, k_old, dims, preferred_element_type=jnp.float32) * scale
        s_new = lax.dot_general(q_heads, k_new, dims, preferred_element_type=jnp.float32) * scale
        s_old = jnp.where(key_old < cache_len_ref[i], s_old, -1e30)
        s_new = jnp.where(key_new <= row_t, s_new, -1e30)
        top = jnp.maximum(jnp.max(s_old, axis=1, keepdims=True), jnp.max(s_new, axis=1, keepdims=True))
        e_old = jnp.exp(s_old - top)
        e_new = jnp.exp(s_new - top)
        denom = jnp.sum(e_old, axis=1, keepdims=True) + jnp.sum(e_new, axis=1, keepdims=True)
        w_old = (e_old / denom).astype(jnp.bfloat16)
        w_new = (e_new / denom).astype(jnp.bfloat16)
        mixed = jnp.dot(w_old, v_old, preferred_element_type=jnp.float32) + jnp.dot(
            w_new, v_new, preferred_element_type=jnp.float32
        )
        mixed = mixed.reshape(H, span_slots, width)
        attended = jnp.sum(jnp.where(head_mask, mixed, 0.0), axis=0)
        hid_ref[i * span_slots : (i + 1) * span_slots, :] = (
            resid_ref[i].astype(jnp.float32) + attended
        ).astype(hid_ref.dtype)
    wide_rows = hid_ref[...].astype(jnp.float32)
    normed = (
        wide_rows
        * lax.rsqrt(jnp.mean(wide_rows * wide_rows, axis=-1, keepdims=True) + 1e-06)
        * gain_ref[...]
    ).astype(jnp.bfloat16)
    activated = jax.nn.silu(
        jnp.dot(normed, up_ref[...], preferred_element_type=jnp.float32)
    ).astype(jnp.bfloat16)
    out_ref[...] = (
        wide_rows + jnp.dot(activated, down_ref[...], preferred_element_type=jnp.float32)
    ).astype(out_ref.dtype)


def layer_block(new_qkv, cache_kv, resid, cache_len, ff_gain, w_up, w_down):
    series_here, span_slots, triple = new_qkv.shape
    width = resid.shape[2]
    vmem = pltpu.MemorySpace.VMEM if hasattr(pltpu, "MemorySpace") else pltpu.VMEM
    full = pl.BlockSpec(memory_space=vmem)
    return pl.pallas_call(
        block_kernel,
        in_specs=[pl.BlockSpec(memory_space=pltpu.SMEM)] + [full] * 6,
        out_specs=full,
        out_shape=jax.ShapeDtypeStruct((series_here * span_slots, width), jnp.bfloat16),
        scratch_shapes=[pltpu.VMEM((series_here * span_slots, width), jnp.bfloat16)],
    )(cache_len, new_qkv, cache_kv, resid, ff_gain.reshape(1, width), w_up, w_down)


def local(new_qkv, cache_kv, resid, span_len, cache_len, series_perm, ff_gain, w_up, w_down):
    group_size = lax.axis_size("req")
    me = lax.axis_index("req")
    series_here, span_slots, triple = new_qkv.shape
    width = resid.shape[2]
    layer_out = layer_block(new_qkv, cache_kv, resid, cache_len, ff_gain, w_up, w_down)
    info = jnp.concatenate([span_len, series_perm])
    gathered = lax.all_to_all(
        jnp.broadcast_to(info[None], (group_size, info.shape[0])), "req", 0, 0, tiled=True
    )
    all_len = gathered[:, :series_here].reshape(-1)
    all_perm = gathered[:, series_here:].reshape(-1)
    series_total = all_len.shape[0]
    earlier = all_perm[None, :] < all_perm[:, None]
    all_start = jnp.sum(jnp.where(earlier, all_len[None, :], 0), axis=1)


    size_x, size_z = 4, 8
    size_y = group_size // (size_x * size_z)
    my_x = me % size_x
    my_z = (me // size_x) % size_z
    my_y = me // (size_x * size_z)

    def shift_pairs(step, size, stride):
        pairs = []
        for q in range(group_size):
            c = (q // stride) % size
            pairs.append((q, q + (((c + step) % size) - c) * stride))
        return pairs

    per_x = span_slots // size_x
    xv = (my_x + jnp.arange(size_x, dtype=jnp.int32))[:, None, None] % size_x
    series_i = jnp.arange(series_here, dtype=jnp.int32)[None, :, None]
    slot_j = jnp.arange(per_x, dtype=jnp.int32)[None, None, :]
    my_start = lax.dynamic_slice(all_start, (me * series_here,), (series_here,))
    t_x = (xv - my_start[None, :, None]) % size_x + size_x * slot_j
    live_x = t_x < span_len[None, :, None]
    col_x = jnp.where(live_x, series_i * span_slots + t_x, -1).reshape(-1)
    rows_here = series_here * span_slots
    pick_x = (col_x[:, None] == jnp.arange(rows_here, dtype=jnp.int32)[None, :]).astype(jnp.bfloat16)
    send_x = jnp.dot(pick_x, layer_out, preferred_element_type=jnp.float32).astype(jnp.bfloat16)
    send_x = send_x.reshape(size_x, series_here * per_x, width)
    recv_x = [send_x[0]] + [
        lax.ppermute(send_x[k], "req", shift_pairs(k, size_x, 1)) for k in range(1, size_x)
    ]
    recv_x = jnp.concatenate(recv_x, axis=0)

    def source_of(src_y, src_z, src_x, i):
        pos = (src_y * (size_z * size_x) + src_z * size_x + src_x) * series_here + i
        st = jnp.take(all_start, pos)
        ln = jnp.take(all_len, pos)
        t0 = (my_x - st) % size_x
        base = (st + t0) // size_x
        return st, ln, t0, base

    kx = jnp.arange(size_x, dtype=jnp.int32)[:, None]
    ii = jnp.arange(series_here, dtype=jnp.int32)[None, :]
    _, _, _, base_b = source_of(my_y, my_z, (my_x - kx) % size_x, ii)
    kz = jnp.arange(size_z, dtype=jnp.int32)[:, None, None]
    zv = (my_z + kz) % size_z
    j_b = (zv - base_b[None]) % size_z
    col_z = (kx[None] * (series_here * per_x) + ii[None] * per_x + j_b).reshape(-1)
    pick_z = (col_z[:, None] == jnp.arange(rows_here, dtype=jnp.int32)[None, :]).astype(jnp.bfloat16)
    send_z = jnp.dot(pick_z, recv_x, preferred_element_type=jnp.float32).astype(jnp.bfloat16)
    send_z = send_z.reshape(size_z, size_x * series_here, width)
    recv_z = [send_z[0]] + [
        lax.ppermute(send_z[k], "req", shift_pairs(k, size_z, size_x)) for k in range(1, size_z)
    ]
    recv_z = jnp.concatenate(recv_z, axis=0)

    recv_y = [recv_z] + [
        lax.ppermute(recv_z, "req", shift_pairs(k, size_y, size_x * size_z)) for k in range(1, size_y)
    ]
    recv_y = jnp.concatenate(recv_y, axis=0)

    ky = jnp.arange(size_y, dtype=jnp.int32)[:, None, None, None]
    kz4 = jnp.arange(size_z, dtype=jnp.int32)[None, :, None, None]
    kx4 = jnp.arange(size_x, dtype=jnp.int32)[None, None, :, None]
    ii4 = jnp.arange(series_here, dtype=jnp.int32)[None, None, None, :]
    st, ln, t0, base = source_of((my_y - ky) % size_y, (my_z - kz4) % size_z, (my_x - kx4) % size_x, ii4)
    t_f = t0 + size_x * ((my_z - base) % size_z)
    g_f = st + t_f
    live_f = (t_f < ln) & (g_f % group_size == me)
    row_f = jnp.where(live_f, g_f // group_size, -1).reshape(-1)
    gather = (row_f[None, :] == jnp.arange(rows_here, dtype=jnp.int32)[:, None]).astype(jnp.bfloat16)
    result = jnp.dot(gather, recv_y, preferred_element_type=jnp.float32)
    return result.astype(jnp.bfloat16)


def solution(mesh):
    in_specs = (
        P(("grp", "req"), None, None),
        P(("grp", "req"), None, None),
        P(("grp", "req"), None, None),
        P(("grp", "req")),
        P(("grp", "req")),
        P(("grp", "req")),
        P(),
        P(),
        P(),
    )
    out_specs = P(("grp", "req"), None)
    return jax.shard_map(local, mesh=mesh, in_specs=in_specs, out_specs=out_specs, check_vma=False)
```

```python
import jax
import jax.numpy as jnp
from jax import lax
from jax.experimental import pallas as pl
from jax.experimental.pallas import tpu as pltpu
from jax.sharding import PartitionSpec as P

H = 16


def block_kernel(cache_len_ref, qkv_ref, cache_ref, resid_ref, gain_ref, up_ref, down_ref, out_ref, hid_ref):
    series_here, span_slots = qkv_ref.shape[0], qkv_ref.shape[1]
    cache_slots = cache_ref.shape[1]
    width = resid_ref.shape[2]
    head_size = width // H
    col_head = lax.broadcasted_iota(jnp.int32, (H, 1, width), 2) // head_size
    head_id = lax.broadcasted_iota(jnp.int32, (H, 1, width), 0)
    head_mask = col_head == head_id
    dims = (((1,), (1,)), ((), ()))
    scale = head_size ** (-0.5)
    rows = H * span_slots
    row_t = lax.broadcasted_iota(jnp.int32, (rows, span_slots), 0) % span_slots
    key_new = lax.broadcasted_iota(jnp.int32, (rows, span_slots), 1)
    key_old = lax.broadcasted_iota(jnp.int32, (rows, cache_slots), 1)
    for i in range(series_here):
        q = qkv_ref[i, :, 0:width]
        k_new = qkv_ref[i, :, width : 2 * width]
        v_new = qkv_ref[i, :, 2 * width : 3 * width]
        k_old = cache_ref[i, :, 0:width]
        v_old = cache_ref[i, :, width : 2 * width]
        q_heads = jnp.where(head_mask, q[None], jnp.zeros((), q.dtype)).reshape(rows, width)
        s_old = lax.dot_general(q_heads, k_old, dims, preferred_element_type=jnp.float32) * scale
        s_new = lax.dot_general(q_heads, k_new, dims, preferred_element_type=jnp.float32) * scale
        s_old = jnp.where(key_old < cache_len_ref[i], s_old, -1e30)
        s_new = jnp.where(key_new <= row_t, s_new, -1e30)
        top = jnp.maximum(jnp.max(s_old, axis=1, keepdims=True), jnp.max(s_new, axis=1, keepdims=True))
        e_old = jnp.exp(s_old - top)
        e_new = jnp.exp(s_new - top)
        denom = jnp.sum(e_old, axis=1, keepdims=True) + jnp.sum(e_new, axis=1, keepdims=True)
        w_old = (e_old / denom).astype(jnp.bfloat16)
        w_new = (e_new / denom).astype(jnp.bfloat16)
        mixed = jnp.dot(w_old, v_old, preferred_element_type=jnp.float32) + jnp.dot(
            w_new, v_new, preferred_element_type=jnp.float32
        )
        mixed = mixed.reshape(H, span_slots, width)
        attended = jnp.sum(jnp.where(head_mask, mixed, 0.0), axis=0)
        hid_ref[i * span_slots : (i + 1) * span_slots, :] = (
            resid_ref[i].astype(jnp.float32) + attended
        ).astype(hid_ref.dtype)
    wide_rows = hid_ref[...].astype(jnp.float32)
    normed = (
        wide_rows
        * lax.rsqrt(jnp.mean(wide_rows * wide_rows, axis=-1, keepdims=True) + 1e-06)
        * gain_ref[...]
    ).astype(jnp.bfloat16)
    activated = jax.nn.silu(
        jnp.dot(normed, up_ref[...], preferred_element_type=jnp.float32)
    ).astype(jnp.bfloat16)
    out_ref[...] = (
        wide_rows + jnp.dot(activated, down_ref[...], preferred_element_type=jnp.float32)
    ).astype(out_ref.dtype)


def layer_block(new_qkv, cache_kv, resid, cache_len, ff_gain, w_up, w_down):
    series_here, span_slots, triple = new_qkv.shape
    width = resid.shape[2]
    vmem = pltpu.MemorySpace.VMEM if hasattr(pltpu, "MemorySpace") else pltpu.VMEM
    full = pl.BlockSpec(memory_space=vmem)
    return pl.pallas_call(
        block_kernel,
        in_specs=[pl.BlockSpec(memory_space=pltpu.SMEM)] + [full] * 6,
        out_specs=full,
        out_shape=jax.ShapeDtypeStruct((series_here * span_slots, width), jnp.bfloat16),
        scratch_shapes=[pltpu.VMEM((series_here * span_slots, width), jnp.bfloat16)],
    )(cache_len, new_qkv, cache_kv, resid, ff_gain.reshape(1, width), w_up, w_down)


REQ = ("y", "z", "x")


def local(new_qkv, cache_kv, resid, span_len, cache_len, series_perm, ff_gain, w_up, w_down):
    group_size = lax.axis_size(REQ)
    me = lax.axis_index(REQ)
    series_here, span_slots, triple = new_qkv.shape
    width = resid.shape[2]
    layer_out = layer_block(new_qkv, cache_kv, resid, cache_len, ff_gain, w_up, w_down)
    info = jnp.concatenate([span_len, series_perm])
    gathered = lax.all_to_all(
        jnp.broadcast_to(info[None], (group_size, info.shape[0])), REQ, 0, 0, tiled=True
    )
    all_len = gathered[:, :series_here].reshape(-1)
    all_perm = gathered[:, series_here:].reshape(-1)
    series_total = all_len.shape[0]
    earlier = all_perm[None, :] < all_perm[:, None]
    all_start = jnp.sum(jnp.where(earlier, all_len[None, :], 0), axis=1)


    size_x, size_z, size_y = lax.axis_size("x"), lax.axis_size("z"), lax.axis_size("y")
    my_x = lax.axis_index("x")
    my_z = lax.axis_index("z")
    my_y = lax.axis_index("y")

    def rotate(blocks, axis, size, me_here):
        blocks = jnp.roll(blocks, me_here, axis=0)
        got = lax.all_to_all(blocks, axis, 0, 0, tiled=True)
        return jnp.roll(got[::-1], me_here + 1, axis=0)

    per_x = span_slots // size_x
    xv = (my_x + jnp.arange(size_x, dtype=jnp.int32))[:, None, None] % size_x
    series_i = jnp.arange(series_here, dtype=jnp.int32)[None, :, None]
    slot_j = jnp.arange(per_x, dtype=jnp.int32)[None, None, :]
    my_start = lax.dynamic_slice(all_start, (me * series_here,), (series_here,))
    t_x = (xv - my_start[None, :, None]) % size_x + size_x * slot_j
    live_x = t_x < span_len[None, :, None]
    col_x = jnp.where(live_x, series_i * span_slots + t_x, -1).reshape(-1)
    rows_here = series_here * span_slots
    pick_x = (col_x[:, None] == jnp.arange(rows_here, dtype=jnp.int32)[None, :]).astype(jnp.bfloat16)
    send_x = jnp.dot(pick_x, layer_out, preferred_element_type=jnp.float32).astype(jnp.bfloat16)
    send_x = send_x.reshape(size_x, series_here * per_x, width)
    recv_x = rotate(send_x, "x", size_x, my_x).reshape(-1, width)

    def source_of(src_y, src_z, src_x, i):
        pos = (src_y * (size_z * size_x) + src_z * size_x + src_x) * series_here + i
        every = jnp.arange(all_start.shape[0], dtype=jnp.int32)
        hit = pos[..., None] == every
        st = jnp.sum(jnp.where(hit, all_start, 0), axis=-1)
        ln = jnp.sum(jnp.where(hit, all_len, 0), axis=-1)
        t0 = (my_x - st) % size_x
        base = (st + t0) // size_x
        return st, ln, t0, base

    kx = jnp.arange(size_x, dtype=jnp.int32)[:, None]
    ii = jnp.arange(series_here, dtype=jnp.int32)[None, :]
    _, _, _, base_b = source_of(my_y, my_z, (my_x - kx) % size_x, ii)
    kz = jnp.arange(size_z, dtype=jnp.int32)[:, None, None]
    zv = (my_z + kz) % size_z
    j_b = (zv - base_b[None]) % size_z
    col_z = (kx[None] * (series_here * per_x) + ii[None] * per_x + j_b).reshape(-1)
    pick_z = (col_z[:, None] == jnp.arange(rows_here, dtype=jnp.int32)[None, :]).astype(jnp.bfloat16)
    send_z = jnp.dot(pick_z, recv_x, preferred_element_type=jnp.float32).astype(jnp.bfloat16)
    send_z = send_z.reshape(size_z, size_x * series_here, width)
    recv_z = rotate(send_z, "z", size_z, my_z).reshape(-1, width)

    recv_y = rotate(
        jnp.broadcast_to(recv_z[None], (size_y,) + recv_z.shape), "y", size_y, my_y
    ).reshape(-1, width)

    ky = jnp.arange(size_y, dtype=jnp.int32)[:, None, None, None]
    kz4 = jnp.arange(size_z, dtype=jnp.int32)[None, :, None, None]
    kx4 = jnp.arange(size_x, dtype=jnp.int32)[None, None, :, None]
    ii4 = jnp.arange(series_here, dtype=jnp.int32)[None, None, None, :]
    st, ln, t0, base = source_of((my_y - ky) % size_y, (my_z - kz4) % size_z, (my_x - kx4) % size_x, ii4)
    t_f = t0 + size_x * ((my_z - base) % size_z)
    g_f = st + t_f
    live_f = (t_f < ln) & (g_f % group_size == me)
    row_f = jnp.where(live_f, g_f // group_size, -1).reshape(-1)
    gather = (row_f[None, :] == jnp.arange(rows_here, dtype=jnp.int32)[:, None]).astype(jnp.bfloat16)
    result = jnp.dot(gather, recv_y, preferred_element_type=jnp.float32)
    return result.astype(jnp.bfloat16)


def solution(mesh):
    grp = mesh.shape["grp"]
    req = mesh.shape["req"]
    fine = jax.sharding.Mesh(mesh.devices.reshape(grp, req // 32, 8, 4), ("grp",) + REQ)
    rows = ("grp",) + REQ
    in_specs = (
        P(rows, None, None),
        P(rows, None, None),
        P(rows, None, None),
        P(rows),
        P(rows),
        P(rows),
        P(),
        P(),
        P(),
    )
    out_specs = P(rows, None)
    return jax.shard_map(local, mesh=fine, in_specs=in_specs, out_specs=out_specs, check_vma=False)
```

```python
import jax
import jax.numpy as jnp
from jax import lax
from jax.experimental import pallas as pl
from jax.experimental.pallas import tpu as pltpu
from jax.sharding import PartitionSpec as P

H = 16


def block_kernel(cache_len_ref, qkv_ref, cache_ref, resid_ref, gain_ref, up_hbm, down_hbm, out_ref,
                 hid_ref, up_ref, down_ref, sem):
    series_here, span_slots = qkv_ref.shape[0], qkv_ref.shape[1]
    cache_slots = cache_ref.shape[1]
    width = resid_ref.shape[2]
    head_size = width // H
    up_copy = pltpu.make_async_copy(up_hbm, up_ref, sem.at[0])
    down_copy = pltpu.make_async_copy(down_hbm, down_ref, sem.at[1])
    up_copy.start()
    down_copy.start()
    group = 8 if H % 8 == 0 and (8 * head_size) % 128 == 0 else H
    group_w = group * head_size
    col_head = lax.broadcasted_iota(jnp.int32, (group, 1, group_w), 2) // head_size
    head_id = lax.broadcasted_iota(jnp.int32, (group, 1, group_w), 0)
    head_mask = col_head == head_id
    dims = (((1,), (1,)), ((), ()))
    scale = head_size ** (-0.5)
    rows = group * span_slots
    row_t = lax.broadcasted_iota(jnp.int32, (rows, span_slots), 0) % span_slots
    key_new = lax.broadcasted_iota(jnp.int32, (rows, span_slots), 1)
    key_old = lax.broadcasted_iota(jnp.int32, (rows, cache_slots), 1)
    for i in range(series_here):
        old_visible = key_old < cache_len_ref[i]
        for g in range(H // group):
            lo = g * group_w
            q = qkv_ref[i, :, lo : lo + group_w]
            k_new = qkv_ref[i, :, width + lo : width + lo + group_w]
            v_new = qkv_ref[i, :, 2 * width + lo : 2 * width + lo + group_w]
            k_old = cache_ref[i, :, lo : lo + group_w]
            v_old = cache_ref[i, :, width + lo : width + lo + group_w]
            q_heads = jnp.where(head_mask, q[None], jnp.zeros((), q.dtype)).reshape(rows, group_w)
            s_old = lax.dot_general(q_heads, k_old, dims, preferred_element_type=jnp.float32) * scale
            s_new = lax.dot_general(q_heads, k_new, dims, preferred_element_type=jnp.float32) * scale
            s_old = jnp.where(old_visible, s_old, -1e30)
            s_new = jnp.where(key_new <= row_t, s_new, -1e30)
            top = jnp.maximum(jnp.max(s_old, axis=1, keepdims=True), jnp.max(s_new, axis=1, keepdims=True))
            e_old = jnp.exp(s_old - top)
            e_new = jnp.exp(s_new - top)
            denom = jnp.sum(e_old, axis=1, keepdims=True) + jnp.sum(e_new, axis=1, keepdims=True)
            w_old = (e_old / denom).astype(jnp.bfloat16)
            w_new = (e_new / denom).astype(jnp.bfloat16)
            mixed = jnp.dot(w_old, v_old, preferred_element_type=jnp.float32) + jnp.dot(
                w_new, v_new, preferred_element_type=jnp.float32
            )
            mixed = mixed.reshape(group, span_slots, group_w)
            attended = jnp.sum(jnp.where(head_mask, mixed, 0.0), axis=0)
            hid_ref[i * span_slots : (i + 1) * span_slots, lo : lo + group_w] = (
                resid_ref[i, :, lo : lo + group_w].astype(jnp.float32) + attended
            ).astype(hid_ref.dtype)
    wide_rows = hid_ref[...].astype(jnp.float32)
    normed = (
        wide_rows
        * lax.rsqrt(jnp.mean(wide_rows * wide_rows, axis=-1, keepdims=True) + 1e-06)
        * gain_ref[...]
    ).astype(jnp.bfloat16)
    up_copy.wait()
    activated = jax.nn.silu(
        jnp.dot(normed, up_ref[...], preferred_element_type=jnp.float32)
    ).astype(jnp.bfloat16)
    down_copy.wait()
    out_ref[...] = (
        wide_rows + jnp.dot(activated, down_ref[...], preferred_element_type=jnp.float32)
    ).astype(out_ref.dtype)


def layer_block(new_qkv, cache_kv, resid, cache_len, ff_gain, w_up, w_down):
    series_here, span_slots, triple = new_qkv.shape
    width = resid.shape[2]
    vmem = pltpu.MemorySpace.VMEM if hasattr(pltpu, "MemorySpace") else pltpu.VMEM
    full = pl.BlockSpec(memory_space=vmem)
    anywhere = pl.BlockSpec(memory_space=pl.ANY)
    return pl.pallas_call(
        block_kernel,
        in_specs=[pl.BlockSpec(memory_space=pltpu.SMEM)] + [full] * 4 + [anywhere] * 2,
        out_specs=full,
        out_shape=jax.ShapeDtypeStruct((series_here * span_slots, width), jnp.bfloat16),
        scratch_shapes=[
            pltpu.VMEM((series_here * span_slots, width), jnp.bfloat16),
            pltpu.VMEM(w_up.shape, w_up.dtype),
            pltpu.VMEM(w_down.shape, w_down.dtype),
            pltpu.SemaphoreType.DMA((2,)),
        ],
    )(cache_len, new_qkv, cache_kv, resid, ff_gain.reshape(1, width), w_up, w_down)


def local(new_qkv, cache_kv, resid, span_len, cache_len, series_perm, ff_gain, w_up, w_down):
    group_size = lax.axis_size("req")
    me = lax.axis_index("req")
    series_here, span_slots, triple = new_qkv.shape
    width = resid.shape[2]
    layer_out = layer_block(new_qkv, cache_kv, resid, cache_len, ff_gain, w_up, w_down)
    info = jnp.concatenate([span_len, series_perm])
    gathered = lax.all_to_all(
        jnp.broadcast_to(info[None], (group_size, info.shape[0])), "req", 0, 0, tiled=True
    )
    all_len = gathered[:, :series_here].reshape(-1)
    all_perm = gathered[:, series_here:].reshape(-1)
    series_total = all_len.shape[0]
    earlier = all_perm[None, :] < all_perm[:, None]
    all_start = jnp.sum(jnp.where(earlier, all_len[None, :], 0), axis=1)


    my_start = lax.dynamic_slice(all_start, (me * series_here,), (series_here,))
    target = jnp.arange(group_size, dtype=jnp.int32)[None, :, None]
    slot = jnp.arange(span_slots, dtype=jnp.int32)[None, None, :]
    my_offset = (target - my_start[:, None, None]) % group_size
    pick = (my_offset == slot) & (slot < span_len[:, None, None])
    same = jnp.arange(series_here)[:, None] == jnp.arange(series_here)[None, :]
    pick = pick.transpose(1, 0, 2)[:, :, None, :] & same[None, :, :, None]
    pick = pick.reshape(group_size * series_here, series_here * span_slots).astype(jnp.bfloat16)

    src_start = all_start.reshape(group_size, series_here)
    src_len = all_len.reshape(group_size, series_here)
    src_t = (me - src_start) % group_size
    src_row = (src_start + src_t) // group_size
    src_row = jnp.where(src_t < src_len, src_row, -1)
    rows_here = series_here * span_slots
    out_row = jnp.arange(rows_here, dtype=jnp.int32)[:, None]
    placed = lax.dot_general(
        pick.reshape(group_size, series_here, -1),
        layer_out,
        (((2,), (0,)), ((), ())),
        preferred_element_type=jnp.float32,
    ).astype(jnp.bfloat16)
    arrived = lax.all_to_all(placed, "req", 0, 0, tiled=True)
    gather = (src_row.reshape(1, -1) == out_row).astype(jnp.bfloat16)
    result = jnp.dot(gather, arrived.reshape(-1, width), preferred_element_type=jnp.float32)
    return result.astype(jnp.bfloat16)


def solution(mesh):
    in_specs = (
        P(("grp", "req"), None, None),
        P(("grp", "req"), None, None),
        P(("grp", "req"), None, None),
        P(("grp", "req")),
        P(("grp", "req")),
        P(("grp", "req")),
        P(),
        P(),
        P(),
    )
    out_specs = P(("grp", "req"), None)
    return jax.shard_map(local, mesh=mesh, in_specs=in_specs, out_specs=out_specs, check_vma=False)
```

```python
import jax
import jax.numpy as jnp
from jax import lax
from jax.experimental import pallas as pl
from jax.experimental.pallas import tpu as pltpu
from jax.sharding import PartitionSpec as P

H = 16


def block_kernel(cache_len_ref, qkv_ref, cache_ref, resid_ref, gain_ref, up_hbm, down_hbm, out_ref,
                 hid_ref, up_ref, down_ref, sem):
    series_here, span_slots = qkv_ref.shape[0], qkv_ref.shape[1]
    cache_slots = cache_ref.shape[1]
    width = resid_ref.shape[2]
    head_size = width // H
    up_copy = pltpu.make_async_copy(up_hbm, up_ref, sem.at[0])
    down_copy = pltpu.make_async_copy(down_hbm, down_ref, sem.at[1])
    up_copy.start()
    down_copy.start()
    group = 8 if H % 8 == 0 and (8 * head_size) % 128 == 0 else H
    group_w = group * head_size
    col_head = lax.broadcasted_iota(jnp.int32, (group, 1, group_w), 2) // head_size
    head_id = lax.broadcasted_iota(jnp.int32, (group, 1, group_w), 0)
    head_mask = col_head == head_id
    dims = (((1,), (1,)), ((), ()))
    scale = head_size ** (-0.5)
    rows = group * span_slots
    row_t = lax.broadcasted_iota(jnp.int32, (rows, span_slots), 0) % span_slots
    key_new = lax.broadcasted_iota(jnp.int32, (rows, span_slots), 1)
    key_old = lax.broadcasted_iota(jnp.int32, (rows, cache_slots), 1)
    for i in range(series_here):
        old_visible = key_old < cache_len_ref[i]
        for g in range(H // group):
            lo = g * group_w
            q = qkv_ref[i, :, lo : lo + group_w]
            k_new = qkv_ref[i, :, width + lo : width + lo + group_w]
            v_new = qkv_ref[i, :, 2 * width + lo : 2 * width + lo + group_w]
            k_old = cache_ref[i, :, lo : lo + group_w]
            v_old = cache_ref[i, :, width + lo : width + lo + group_w]
            q_heads = jnp.where(head_mask, q[None], jnp.zeros((), q.dtype)).reshape(rows, group_w)
            s_old = lax.dot_general(q_heads, k_old, dims, preferred_element_type=jnp.float32) * scale
            s_new = lax.dot_general(q_heads, k_new, dims, preferred_element_type=jnp.float32) * scale
            s_old = jnp.where(old_visible, s_old, -1e30)
            s_new = jnp.where(key_new <= row_t, s_new, -1e30)
            top = jnp.maximum(jnp.max(s_old, axis=1, keepdims=True), jnp.max(s_new, axis=1, keepdims=True))
            e_old = jnp.exp(s_old - top)
            e_new = jnp.exp(s_new - top)
            denom = jnp.sum(e_old, axis=1, keepdims=True) + jnp.sum(e_new, axis=1, keepdims=True)
            w_old = (e_old / denom).astype(jnp.bfloat16)
            w_new = (e_new / denom).astype(jnp.bfloat16)
            mixed = jnp.dot(w_old, v_old, preferred_element_type=jnp.float32) + jnp.dot(
                w_new, v_new, preferred_element_type=jnp.float32
            )
            mixed = mixed.reshape(group, span_slots, group_w)
            attended = jnp.sum(jnp.where(head_mask, mixed, 0.0), axis=0)
            hid_ref[i * span_slots : (i + 1) * span_slots, lo : lo + group_w] = (
                resid_ref[i, :, lo : lo + group_w].astype(jnp.float32) + attended
            ).astype(hid_ref.dtype)
    wide_rows = hid_ref[...].astype(jnp.float32)
    normed = (
        wide_rows
        * lax.rsqrt(jnp.mean(wide_rows * wide_rows, axis=-1, keepdims=True) + 1e-06)
        * gain_ref[...].reshape(1, width)
    ).astype(jnp.bfloat16)
    up_copy.wait()
    activated = jax.nn.silu(
        jnp.dot(normed, up_ref[...], preferred_element_type=jnp.float32)
    ).astype(jnp.bfloat16)
    down_copy.wait()
    out_ref[...] = (
        wide_rows + jnp.dot(activated, down_ref[...], preferred_element_type=jnp.float32)
    ).astype(out_ref.dtype)


def layer_block(new_qkv, cache_kv, resid, cache_len, ff_gain, w_up, w_down):
    series_here, span_slots, triple = new_qkv.shape
    width = resid.shape[2]
    vmem = pltpu.MemorySpace.VMEM if hasattr(pltpu, "MemorySpace") else pltpu.VMEM
    full = pl.BlockSpec(memory_space=vmem)
    anywhere = pl.BlockSpec(memory_space=pl.ANY)
    return pl.pallas_call(
        block_kernel,
        in_specs=[pl.BlockSpec(memory_space=pltpu.SMEM)] + [full] * 4 + [anywhere] * 2,
        out_specs=full,
        out_shape=jax.ShapeDtypeStruct((series_here * span_slots, width), jnp.bfloat16),
        scratch_shapes=[
            pltpu.VMEM((series_here * span_slots, width), jnp.bfloat16),
            pltpu.VMEM(w_up.shape, w_up.dtype),
            pltpu.VMEM(w_down.shape, w_down.dtype),
            pltpu.SemaphoreType.DMA((2,)),
        ],
    )(cache_len, new_qkv, cache_kv, resid, ff_gain, w_up, w_down)


def local(new_qkv, cache_kv, resid, span_len, cache_len, series_perm, ff_gain, w_up, w_down):
    group_size = lax.axis_size("req")
    me = lax.axis_index("req")
    series_here, span_slots, triple = new_qkv.shape
    width = resid.shape[2]
    layer_out = layer_block(new_qkv, cache_kv, resid, cache_len, ff_gain, w_up, w_down)
    info = jnp.concatenate(
        [jnp.broadcast_to(span_len[None], (group_size, series_here)),
         jnp.broadcast_to(series_perm[None], (group_size, series_here))], axis=1
    )
    gathered = lax.all_to_all(info, "req", 0, 0, tiled=True)
    all_len = gathered[:, :series_here].reshape(-1)
    all_perm = gathered[:, series_here:].reshape(-1)
    series_total = all_len.shape[0]
    earlier = all_perm[None, :] < all_perm[:, None]
    all_start = jnp.sum(jnp.where(earlier, all_len[None, :], 0), axis=1)


    my_start = lax.dynamic_slice(all_start, (me * series_here,), (series_here,))
    target = jnp.arange(group_size, dtype=jnp.int32)[None, :, None]
    slot = jnp.arange(span_slots, dtype=jnp.int32)[None, None, :]
    my_offset = (target - my_start[:, None, None]) % group_size
    pick = (my_offset == slot) & (slot < span_len[:, None, None])
    half = width // 2
    same = jnp.arange(series_here)[:, None] == jnp.arange(series_here)[None, :]
    pick = pick.transpose(1, 0, 2)[:, :, None, :] & same[None, :, :, None]
    pick = pick.reshape(group_size, series_here, 1, series_here * span_slots)
    halves = jnp.arange(2)[None, None, :, None]
    rows_here = series_here * span_slots
    placed = 0
    for h in range(2):
        pick_h = (pick & (halves == h)).reshape(-1, rows_here).astype(jnp.bfloat16)
        placed = placed + jnp.dot(
            pick_h, layer_out[:, h * half : (h + 1) * half], preferred_element_type=jnp.float32
        )
    placed = placed.astype(jnp.bfloat16)
    arrived = lax.all_to_all(placed, "req", 0, 0, tiled=True)

    src_start = all_start.reshape(group_size, series_here)
    src_len = all_len.reshape(group_size, series_here)
    src_t = (me - src_start) % group_size
    src_row = (src_start + src_t) // group_size
    src_row = jnp.where(src_t < src_len, src_row, -1)
    out_row = jnp.arange(rows_here, dtype=jnp.int32)[:, None, None, None]
    hit = src_row[None, :, :, None] == out_row
    result = jnp.concatenate(
        [
            jnp.dot(
                (hit & (halves.reshape(1, 1, 1, 2) == h)).reshape(rows_here, -1).astype(jnp.bfloat16),
                arrived,
                preferred_element_type=jnp.float32,
            )
            for h in range(2)
        ],
        axis=1,
    )
    return result.astype(jnp.bfloat16)


def solution(mesh):
    in_specs = (
        P(("grp", "req"), None, None),
        P(("grp", "req"), None, None),
        P(("grp", "req"), None, None),
        P(("grp", "req")),
        P(("grp", "req")),
        P(("grp", "req")),
        P(),
        P(),
        P(),
    )
    out_specs = P(("grp", "req"), None)
    return jax.shard_map(local, mesh=mesh, in_specs=in_specs, out_specs=out_specs, check_vma=False)
```

```python
import jax
import jax.numpy as jnp
from jax import lax
from jax.experimental import pallas as pl
from jax.experimental.pallas import tpu as pltpu
from jax.sharding import PartitionSpec as P

H = 16


def block_kernel(cache_len_ref, qkv_ref, cache_ref, resid_ref, gain_ref, up_hbm, down_hbm, out_ref,
                 hid_ref, up_ref, down_ref, sem):
    series_here, span_slots = qkv_ref.shape[0], qkv_ref.shape[1]
    cache_slots = cache_ref.shape[1]
    width = resid_ref.shape[2]
    head_size = width // H
    up_copy = pltpu.make_async_copy(up_hbm, up_ref, sem.at[0])
    down_copy = pltpu.make_async_copy(down_hbm, down_ref, sem.at[1])
    up_copy.start()
    down_copy.start()
    group = 8 if H % 8 == 0 and (8 * head_size) % 128 == 0 else H
    group_w = group * head_size
    col_head = lax.broadcasted_iota(jnp.int32, (group, 1, group_w), 2) // head_size
    head_id = lax.broadcasted_iota(jnp.int32, (group, 1, group_w), 0)
    head_mask = col_head == head_id
    dims = (((1,), (1,)), ((), ()))
    scale = head_size ** (-0.5)
    rows = group * span_slots
    row_t = lax.broadcasted_iota(jnp.int32, (rows, span_slots), 0) % span_slots
    key_new = lax.broadcasted_iota(jnp.int32, (rows, span_slots), 1)
    key_old = lax.broadcasted_iota(jnp.int32, (rows, cache_slots), 1)
    for i in range(series_here):
        old_visible = key_old < cache_len_ref[i]
        for g in range(H // group):
            lo = g * group_w
            q = qkv_ref[i, :, lo : lo + group_w]
            k_new = qkv_ref[i, :, width + lo : width + lo + group_w]
            v_new = qkv_ref[i, :, 2 * width + lo : 2 * width + lo + group_w]
            k_old = cache_ref[i, :, lo : lo + group_w]
            v_old = cache_ref[i, :, width + lo : width + lo + group_w]
            q_heads = jnp.where(head_mask, q[None], jnp.zeros((), q.dtype)).reshape(rows, group_w)
            s_old = lax.dot_general(q_heads, k_old, dims, preferred_element_type=jnp.float32) * scale
            s_new = lax.dot_general(q_heads, k_new, dims, preferred_element_type=jnp.float32) * scale
            s_old = jnp.where(old_visible, s_old, -1e30)
            s_new = jnp.where(key_new <= row_t, s_new, -1e30)
            top = jnp.maximum(jnp.max(s_old, axis=1, keepdims=True), jnp.max(s_new, axis=1, keepdims=True))
            e_old = jnp.exp(s_old - top)
            e_new = jnp.exp(s_new - top)
            denom = jnp.sum(e_old, axis=1, keepdims=True) + jnp.sum(e_new, axis=1, keepdims=True)
            w_old = (e_old / denom).astype(jnp.bfloat16)
            w_new = (e_new / denom).astype(jnp.bfloat16)
            mixed = jnp.dot(w_old, v_old, preferred_element_type=jnp.float32) + jnp.dot(
                w_new, v_new, preferred_element_type=jnp.float32
            )
            mixed = mixed.reshape(group, span_slots, group_w)
            attended = jnp.sum(jnp.where(head_mask, mixed, 0.0), axis=0)
            hid_ref[i * span_slots : (i + 1) * span_slots, lo : lo + group_w] = (
                resid_ref[i, :, lo : lo + group_w].astype(jnp.float32) + attended
            ).astype(hid_ref.dtype)
    wide_rows = hid_ref[...].astype(jnp.float32)
    normed = (
        wide_rows
        * lax.rsqrt(jnp.mean(wide_rows * wide_rows, axis=-1, keepdims=True) + 1e-06)
        * gain_ref[...].reshape(1, width)
    ).astype(jnp.bfloat16)
    up_copy.wait()
    activated = jax.nn.silu(
        jnp.dot(normed, up_ref[...], preferred_element_type=jnp.float32)
    ).astype(jnp.bfloat16)
    down_copy.wait()
    out_ref[...] = (
        wide_rows + jnp.dot(activated, down_ref[...], preferred_element_type=jnp.float32)
    ).astype(out_ref.dtype)


def layer_block(new_qkv, cache_kv, resid, cache_len, ff_gain, w_up, w_down):
    series_here, span_slots, triple = new_qkv.shape
    width = resid.shape[2]
    vmem = pltpu.MemorySpace.VMEM if hasattr(pltpu, "MemorySpace") else pltpu.VMEM
    full = pl.BlockSpec(memory_space=vmem)
    anywhere = pl.BlockSpec(memory_space=pl.ANY)
    return pl.pallas_call(
        block_kernel,
        in_specs=[pl.BlockSpec(memory_space=pltpu.SMEM)] + [full] * 4 + [anywhere] * 2,
        out_specs=full,
        out_shape=jax.ShapeDtypeStruct((series_here * span_slots, width), jnp.bfloat16),
        scratch_shapes=[
            pltpu.VMEM((series_here * span_slots, width), jnp.bfloat16),
            pltpu.VMEM(w_up.shape, w_up.dtype),
            pltpu.VMEM(w_down.shape, w_down.dtype),
            pltpu.SemaphoreType.DMA((2,)),
        ],
    )(cache_len, new_qkv, cache_kv, resid, ff_gain, w_up, w_down)


def send_kernel(start_ref, len_ref, rows_ref, out_ref):
    rows, cols = out_ref.shape[0], rows_ref.shape[0]
    series_here = start_ref.shape[0]
    span_slots = cols // series_here
    half = out_ref.shape[1]
    targets = rows // (2 * series_here)
    r = lax.broadcasted_iota(jnp.int32, (rows, cols), 0)
    c = lax.broadcasted_iota(jnp.int32, (rows, cols), 1)
    d = r // (2 * series_here)
    i = (r // 2) % series_here
    h = r % 2
    start_i = jnp.zeros((rows, cols), jnp.int32)
    len_i = jnp.zeros((rows, cols), jnp.int32)
    for k in range(series_here):
        start_i = jnp.where(i == k, start_ref[k], start_i)
        len_i = jnp.where(i == k, len_ref[k], len_i)
    t = c % span_slots
    hit = (c // span_slots == i) & (t == (d - start_i) % targets) & (t < len_i)
    acc = jnp.zeros((rows, half), jnp.float32)
    for k in range(2):
        pick = jnp.where(hit & (h == k), 1.0, 0.0).astype(jnp.bfloat16)
        acc = acc + jnp.dot(pick, rows_ref[:, k * half : (k + 1) * half], preferred_element_type=jnp.float32)
    out_ref[...] = acc.astype(out_ref.dtype)


def send_block(my_start, span_len, layer_out, targets):
    series_here = my_start.shape[0]
    width = layer_out.shape[1]
    smem = pl.BlockSpec(memory_space=pltpu.SMEM)
    vmem = pltpu.MemorySpace.VMEM if hasattr(pltpu, "MemorySpace") else pltpu.VMEM
    full = pl.BlockSpec(memory_space=vmem)
    return pl.pallas_call(
        send_kernel,
        in_specs=[smem, smem, full],
        out_specs=full,
        out_shape=jax.ShapeDtypeStruct((targets * series_here * 2, width // 2), layer_out.dtype),
    )(my_start, span_len, layer_out)


def local(new_qkv, cache_kv, resid, span_len, cache_len, series_perm, ff_gain, w_up, w_down):
    group_size = lax.axis_size("req")
    me = lax.axis_index("req")
    series_here, span_slots, triple = new_qkv.shape
    width = resid.shape[2]
    layer_out = layer_block(new_qkv, cache_kv, resid, cache_len, ff_gain, w_up, w_down)
    pack = 2 * span_slots
    info = jnp.broadcast_to((series_perm * pack + span_len)[None], (group_size, series_here))
    gathered = lax.all_to_all(info, "req", 0, 0, tiled=True).reshape(-1)
    all_len = gathered % pack
    all_perm = gathered // pack
    series_total = all_len.shape[0]
    earlier = all_perm[None, :] < all_perm[:, None]
    all_start = jnp.sum(jnp.where(earlier, all_len[None, :], 0), axis=1)


    my_start = lax.dynamic_slice(all_start, (me * series_here,), (series_here,))
    rows_here = series_here * span_slots
    half = width // 2
    halves = jnp.arange(2)[None, None, :, None]
    placed = send_block(my_start, span_len, layer_out, group_size)
    arrived = lax.all_to_all(placed, "req", 0, 0, tiled=True)

    src_start = all_start.reshape(group_size, series_here)
    src_len = all_len.reshape(group_size, series_here)
    src_t = (me - src_start) % group_size
    src_row = (src_start + src_t) // group_size
    src_row = jnp.where(src_t < src_len, src_row, -1)
    out_row = jnp.arange(rows_here, dtype=jnp.int32)[:, None, None, None]
    hit = src_row[None, :, :, None] == out_row
    result = jnp.concatenate(
        [
            jnp.dot(
                (hit & (halves.reshape(1, 1, 1, 2) == h)).reshape(rows_here, -1).astype(jnp.bfloat16),
                arrived,
                preferred_element_type=jnp.float32,
            )
            for h in range(2)
        ],
        axis=1,
    )
    return result.astype(jnp.bfloat16)


def solution(mesh):
    in_specs = (
        P(("grp", "req"), None, None),
        P(("grp", "req"), None, None),
        P(("grp", "req"), None, None),
        P(("grp", "req")),
        P(("grp", "req")),
        P(("grp", "req")),
        P(),
        P(),
        P(),
    )
    out_specs = P(("grp", "req"), None)
    return jax.shard_map(local, mesh=mesh, in_specs=in_specs, out_specs=out_specs, check_vma=False)
```

```python
import jax
import jax.numpy as jnp
from jax import lax
from jax.experimental import pallas as pl
from jax.experimental.pallas import tpu as pltpu
from jax.sharding import PartitionSpec as P

H = 16


def block_kernel(cache_len_ref, qkv_ref, cache_ref, resid_ref, gain_ref, up_hbm, down_hbm, out_ref,
                 hid_ref, up_ref, down_ref, sem):
    series_here, span_slots = qkv_ref.shape[0], qkv_ref.shape[1]
    cache_slots = cache_ref.shape[1]
    width = resid_ref.shape[2]
    head_size = width // H
    up_copy = pltpu.make_async_copy(up_hbm, up_ref, sem.at[0])
    down_copy = pltpu.make_async_copy(down_hbm, down_ref, sem.at[1])
    up_copy.start()
    down_copy.start()
    group = 8 if H % 8 == 0 and (8 * head_size) % 128 == 0 else H
    group_w = group * head_size
    col_head = lax.broadcasted_iota(jnp.int32, (group, 1, group_w), 2) // head_size
    head_id = lax.broadcasted_iota(jnp.int32, (group, 1, group_w), 0)
    head_mask = col_head == head_id
    dims = (((1,), (1,)), ((), ()))
    scale = head_size ** (-0.5)
    rows = group * span_slots
    row_t = lax.broadcasted_iota(jnp.int32, (rows, span_slots), 0) % span_slots
    key_new = lax.broadcasted_iota(jnp.int32, (rows, span_slots), 1)
    key_old = lax.broadcasted_iota(jnp.int32, (rows, cache_slots), 1)
    for i in range(series_here):
        old_visible = key_old < cache_len_ref[i]
        for g in range(H // group):
            lo = g * group_w
            q = qkv_ref[i, :, lo : lo + group_w]
            k_new = qkv_ref[i, :, width + lo : width + lo + group_w]
            v_new = qkv_ref[i, :, 2 * width + lo : 2 * width + lo + group_w]
            k_old = cache_ref[i, :, lo : lo + group_w]
            v_old = cache_ref[i, :, width + lo : width + lo + group_w]
            q_heads = jnp.where(head_mask, q[None], jnp.zeros((), q.dtype)).reshape(rows, group_w)
            s_old = lax.dot_general(q_heads, k_old, dims, preferred_element_type=jnp.float32) * scale
            s_new = lax.dot_general(q_heads, k_new, dims, preferred_element_type=jnp.float32) * scale
            s_old = jnp.where(old_visible, s_old, -1e30)
            s_new = jnp.where(key_new <= row_t, s_new, -1e30)
            top = jnp.maximum(jnp.max(s_old, axis=1, keepdims=True), jnp.max(s_new, axis=1, keepdims=True))
            e_old = jnp.exp(s_old - top)
            e_new = jnp.exp(s_new - top)
            denom = jnp.sum(e_old, axis=1, keepdims=True) + jnp.sum(e_new, axis=1, keepdims=True)
            w_old = (e_old / denom).astype(jnp.bfloat16)
            w_new = (e_new / denom).astype(jnp.bfloat16)
            mixed = jnp.dot(w_old, v_old, preferred_element_type=jnp.float32) + jnp.dot(
                w_new, v_new, preferred_element_type=jnp.float32
            )
            mixed = mixed.reshape(group, span_slots, group_w)
            attended = jnp.sum(jnp.where(head_mask, mixed, 0.0), axis=0)
            hid_ref[i * span_slots : (i + 1) * span_slots, lo : lo + group_w] = (
                resid_ref[i, :, lo : lo + group_w].astype(jnp.float32) + attended
            ).astype(hid_ref.dtype)
    wide_rows = hid_ref[...].astype(jnp.float32)
    normed = (
        wide_rows
        * lax.rsqrt(jnp.mean(wide_rows * wide_rows, axis=-1, keepdims=True) + 1e-06)
        * gain_ref[...].reshape(1, width)
    ).astype(jnp.bfloat16)
    up_copy.wait()
    activated = jax.nn.silu(
        jnp.dot(normed, up_ref[...], preferred_element_type=jnp.float32)
    ).astype(jnp.bfloat16)
    down_copy.wait()
    out_ref[...] = (
        wide_rows + jnp.dot(activated, down_ref[...], preferred_element_type=jnp.float32)
    ).astype(out_ref.dtype)


def layer_block(new_qkv, cache_kv, resid, cache_len, ff_gain, w_up, w_down):
    series_here, span_slots, triple = new_qkv.shape
    width = resid.shape[2]
    vmem = pltpu.MemorySpace.VMEM if hasattr(pltpu, "MemorySpace") else pltpu.VMEM
    full = pl.BlockSpec(memory_space=vmem)
    anywhere = pl.BlockSpec(memory_space=pl.ANY)
    return pl.pallas_call(
        block_kernel,
        in_specs=[pl.BlockSpec(memory_space=pltpu.SMEM)] + [full] * 4 + [anywhere] * 2,
        out_specs=full,
        out_shape=jax.ShapeDtypeStruct((series_here * span_slots, width), jnp.bfloat16),
        scratch_shapes=[
            pltpu.VMEM((series_here * span_slots, width), jnp.bfloat16),
            pltpu.VMEM(w_up.shape, w_up.dtype),
            pltpu.VMEM(w_down.shape, w_down.dtype),
            pltpu.SemaphoreType.DMA((2,)),
        ],
    )(cache_len, new_qkv, cache_kv, resid, ff_gain, w_up, w_down)


def local(new_qkv, cache_kv, resid, span_len, cache_len, series_perm, ff_gain, w_up, w_down):
    group_size = lax.axis_size("req")
    me = lax.axis_index("req")
    series_here, span_slots, triple = new_qkv.shape
    width = resid.shape[2]
    layer_out = layer_block(new_qkv, cache_kv, resid, cache_len, ff_gain, w_up, w_down)
    pack = 2 * span_slots
    everyone = ("grp", "req")
    code = (series_perm * pack + span_len).astype(jnp.float32)
    lanes = 128
    own_row = jnp.zeros((lax.axis_size(everyone), lanes), jnp.float32)
    own_row = lax.dynamic_update_slice(
        own_row, jnp.pad(code, (0, lanes - series_here))[None], (lax.axis_index(everyone), 0)
    )
    summed = lax.psum(own_row, everyone)
    summed = lax.dynamic_slice_in_dim(summed, lax.axis_index("grp") * group_size, group_size, 0)
    gathered = summed[:, :series_here].astype(jnp.int32).reshape(-1)
    all_len = gathered % pack
    all_perm = gathered // pack
    series_total = all_len.shape[0]
    earlier = all_perm[None, :] < all_perm[:, None]
    all_start = jnp.sum(jnp.where(earlier, all_len[None, :], 0), axis=1)


    my_start = lax.dynamic_slice(all_start, (me * series_here,), (series_here,))
    target = jnp.arange(group_size, dtype=jnp.int32)[None, :, None]
    slot = jnp.arange(span_slots, dtype=jnp.int32)[None, None, :]
    my_offset = (target - my_start[:, None, None]) % group_size
    pick = (my_offset == slot) & (slot < span_len[:, None, None])
    half = width // 2
    same = jnp.arange(series_here)[:, None] == jnp.arange(series_here)[None, :]
    pick = pick.transpose(1, 0, 2)[:, :, None, :] & same[None, :, :, None]
    pick = pick.reshape(group_size, series_here, 1, series_here * span_slots)
    halves = jnp.arange(2)[None, None, :, None]
    rows_here = series_here * span_slots
    placed = 0
    for h in range(2):
        pick_h = (pick & (halves == h)).reshape(-1, rows_here).astype(jnp.bfloat16)
        placed = placed + jnp.dot(
            pick_h, layer_out[:, h * half : (h + 1) * half], preferred_element_type=jnp.float32
        )
    placed = placed.astype(jnp.bfloat16)
    arrived = lax.all_to_all(placed, "req", 0, 0, tiled=True)

    src_start = all_start.reshape(group_size, series_here)
    src_len = all_len.reshape(group_size, series_here)
    src_t = (me - src_start) % group_size
    src_row = (src_start + src_t) // group_size
    src_row = jnp.where(src_t < src_len, src_row, -1)
    out_row = jnp.arange(rows_here, dtype=jnp.int32)[:, None, None, None]
    hit = src_row[None, :, :, None] == out_row
    result = jnp.concatenate(
        [
            jnp.dot(
                (hit & (halves.reshape(1, 1, 1, 2) == h)).reshape(rows_here, -1).astype(jnp.bfloat16),
                arrived,
                preferred_element_type=jnp.float32,
            )
            for h in range(2)
        ],
        axis=1,
    )
    return result.astype(jnp.bfloat16)


def solution(mesh):
    in_specs = (
        P(("grp", "req"), None, None),
        P(("grp", "req"), None, None),
        P(("grp", "req"), None, None),
        P(("grp", "req")),
        P(("grp", "req")),
        P(("grp", "req")),
        P(),
        P(),
        P(),
    )
    out_specs = P(("grp", "req"), None)
    return jax.shard_map(local, mesh=mesh, in_specs=in_specs, out_specs=out_specs, check_vma=False)
```

```python
import jax
import jax.numpy as jnp
from jax import lax
from jax.experimental import pallas as pl
from jax.experimental.pallas import tpu as pltpu
from jax.sharding import PartitionSpec as P

H = 16


def block_kernel(cache_len_ref, qkv_ref, cache_ref, resid_ref, gain_ref, up_hbm, down_hbm, out_ref,
                 hid_ref, up_ref, down_ref, sem):
    series_here, span_slots = qkv_ref.shape[0], qkv_ref.shape[1]
    cache_slots = cache_ref.shape[1]
    width = resid_ref.shape[2]
    head_size = width // H
    up_copy = pltpu.make_async_copy(up_hbm, up_ref, sem.at[0])
    down_copy = pltpu.make_async_copy(down_hbm, down_ref, sem.at[1])
    up_copy.start()
    down_copy.start()
    group = 8 if H % 8 == 0 and (8 * head_size) % 128 == 0 else H
    group_w = group * head_size
    col_head = lax.broadcasted_iota(jnp.int32, (group, 1, group_w), 2) // head_size
    head_id = lax.broadcasted_iota(jnp.int32, (group, 1, group_w), 0)
    head_mask = col_head == head_id
    dims = (((1,), (1,)), ((), ()))
    scale = head_size ** (-0.5)
    rows = group * span_slots
    row_t = lax.broadcasted_iota(jnp.int32, (rows, span_slots), 0) % span_slots
    key_new = lax.broadcasted_iota(jnp.int32, (rows, span_slots), 1)
    key_old = lax.broadcasted_iota(jnp.int32, (rows, cache_slots), 1)
    for i in range(series_here):
        old_visible = key_old < cache_len_ref[i]
        for g in range(H // group):
            lo = g * group_w
            q = qkv_ref[i, :, lo : lo + group_w]
            k_new = qkv_ref[i, :, width + lo : width + lo + group_w]
            v_new = qkv_ref[i, :, 2 * width + lo : 2 * width + lo + group_w]
            k_old = cache_ref[i, :, lo : lo + group_w]
            v_old = cache_ref[i, :, width + lo : width + lo + group_w]
            q_heads = jnp.where(head_mask, q[None], jnp.zeros((), q.dtype)).reshape(rows, group_w)
            s_old = lax.dot_general(q_heads, k_old, dims, preferred_element_type=jnp.float32) * scale
            s_new = lax.dot_general(q_heads, k_new, dims, preferred_element_type=jnp.float32) * scale
            s_old = jnp.where(old_visible, s_old, -1e30)
            s_new = jnp.where(key_new <= row_t, s_new, -1e30)
            top = jnp.maximum(jnp.max(s_old, axis=1, keepdims=True), jnp.max(s_new, axis=1, keepdims=True))
            e_old = jnp.exp(s_old - top)
            e_new = jnp.exp(s_new - top)
            denom = jnp.sum(e_old, axis=1, keepdims=True) + jnp.sum(e_new, axis=1, keepdims=True)
            w_old = (e_old / denom).astype(jnp.bfloat16)
            w_new = (e_new / denom).astype(jnp.bfloat16)
            mixed = jnp.dot(w_old, v_old, preferred_element_type=jnp.float32) + jnp.dot(
                w_new, v_new, preferred_element_type=jnp.float32
            )
            mixed = mixed.reshape(group, span_slots, group_w)
            attended = jnp.sum(jnp.where(head_mask, mixed, 0.0), axis=0)
            hid_ref[i * span_slots : (i + 1) * span_slots, lo : lo + group_w] = (
                resid_ref[i, :, lo : lo + group_w].astype(jnp.float32) + attended
            ).astype(hid_ref.dtype)
    wide_rows = hid_ref[...].astype(jnp.float32)
    normed = (
        wide_rows
        * lax.rsqrt(jnp.mean(wide_rows * wide_rows, axis=-1, keepdims=True) + 1e-06)
        * gain_ref[...].reshape(1, width)
    ).astype(jnp.bfloat16)
    up_copy.wait()
    activated = jax.nn.silu(
        jnp.dot(normed, up_ref[...], preferred_element_type=jnp.float32)
    ).astype(jnp.bfloat16)
    down_copy.wait()
    out_ref[...] = (
        wide_rows + jnp.dot(activated, down_ref[...], preferred_element_type=jnp.float32)
    ).astype(out_ref.dtype)


def layer_block(new_qkv, cache_kv, resid, cache_len, ff_gain, w_up, w_down):
    series_here, span_slots, triple = new_qkv.shape
    width = resid.shape[2]
    vmem = pltpu.MemorySpace.VMEM if hasattr(pltpu, "MemorySpace") else pltpu.VMEM
    full = pl.BlockSpec(memory_space=vmem)
    anywhere = pl.BlockSpec(memory_space=pl.ANY)
    return pl.pallas_call(
        block_kernel,
        in_specs=[pl.BlockSpec(memory_space=pltpu.SMEM)] + [full] * 4 + [anywhere] * 2,
        out_specs=full,
        out_shape=jax.ShapeDtypeStruct((series_here * span_slots, width), jnp.bfloat16),
        scratch_shapes=[
            pltpu.VMEM((series_here * span_slots, width), jnp.bfloat16),
            pltpu.VMEM(w_up.shape, w_up.dtype),
            pltpu.VMEM(w_down.shape, w_down.dtype),
            pltpu.SemaphoreType.DMA((2,)),
        ],
    )(cache_len, new_qkv, cache_kv, resid, ff_gain, w_up, w_down)


REQ = ("y", "z", "x")
PLANE = ("z", "x")


def local(new_qkv, cache_kv, resid, span_len, cache_len, series_perm, ff_gain, w_up, w_down):
    group_size = lax.axis_size(REQ)
    me = lax.axis_index(REQ)
    plane = lax.axis_size(PLANE)
    series_here, span_slots, triple = new_qkv.shape
    width = resid.shape[2]
    layer_out = layer_block(new_qkv, cache_kv, resid, cache_len, ff_gain, w_up, w_down)
    info = jnp.concatenate(
        [jnp.broadcast_to(span_len[None], (group_size, series_here)),
         jnp.broadcast_to(series_perm[None], (group_size, series_here))], axis=1
    )
    gathered = lax.all_to_all(info, REQ, 0, 0, tiled=True)
    all_len = gathered[:, :series_here].reshape(-1)
    all_perm = gathered[:, series_here:].reshape(-1)
    series_total = all_len.shape[0]
    earlier = all_perm[None, :] < all_perm[:, None]
    all_start = jnp.sum(jnp.where(earlier, all_len[None, :], 0), axis=1)


    my_start = lax.dynamic_slice(all_start, (me * series_here,), (series_here,))
    target = jnp.arange(plane, dtype=jnp.int32)[None, :, None]
    slot = jnp.arange(span_slots, dtype=jnp.int32)[None, None, :]
    my_offset = (target - my_start[:, None, None]) % plane
    pick = (my_offset == slot) & (slot < span_len[:, None, None])
    half = width // 2
    same = jnp.arange(series_here)[:, None] == jnp.arange(series_here)[None, :]
    pick = pick.transpose(1, 0, 2)[:, :, None, :] & same[None, :, :, None]
    pick = pick.reshape(plane, series_here, 1, series_here * span_slots)
    halves = jnp.arange(2)[None, None, :, None]
    rows_here = series_here * span_slots
    placed = 0
    for h in range(2):
        pick_h = (pick & (halves == h)).reshape(-1, rows_here).astype(jnp.bfloat16)
        placed = placed + jnp.dot(
            pick_h, layer_out[:, h * half : (h + 1) * half], preferred_element_type=jnp.float32
        )
    placed = placed.astype(jnp.bfloat16)
    in_plane = lax.all_to_all(placed, PLANE, 0, 0, tiled=True)
    ys = group_size // plane
    arrived = lax.all_to_all(
        jnp.broadcast_to(in_plane[None], (ys,) + in_plane.shape), "y", 0, 0, tiled=True
    ).reshape(-1, in_plane.shape[1])

    src_start = all_start.reshape(group_size, series_here)
    src_len = all_len.reshape(group_size, series_here)
    src_t = (me - src_start) % group_size
    src_row = (src_start + src_t) // group_size
    src_row = jnp.where(src_t < src_len, src_row, -1)
    out_row = jnp.arange(rows_here, dtype=jnp.int32)[:, None, None, None]
    hit = src_row[None, :, :, None] == out_row
    result = jnp.concatenate(
        [
            jnp.dot(
                (hit & (halves.reshape(1, 1, 1, 2) == h)).reshape(rows_here, -1).astype(jnp.bfloat16),
                arrived,
                preferred_element_type=jnp.float32,
            )
            for h in range(2)
        ],
        axis=1,
    )
    return result.astype(jnp.bfloat16)


def solution(mesh):
    grp = mesh.shape["grp"]
    req = mesh.shape["req"]
    fine = jax.sharding.Mesh(mesh.devices.reshape(grp, req // 32, 8, 4), ("grp",) + REQ)
    rows = ("grp",) + REQ
    in_specs = (
        P(rows, None, None),
        P(rows, None, None),
        P(rows, None, None),
        P(rows),
        P(rows),
        P(rows),
        P(),
        P(),
        P(),
    )
    out_specs = P(rows, None)
    return jax.shard_map(local, mesh=fine, in_specs=in_specs, out_specs=out_specs, check_vma=False)
```

```python
import jax
import jax.numpy as jnp
from jax import lax
from jax.experimental import pallas as pl
from jax.experimental.pallas import tpu as pltpu
from jax.sharding import PartitionSpec as P

H = 16


def block_kernel(cache_len_ref, qkv_ref, cache_ref, resid_ref, gain_ref, up_hbm, down_hbm, out_ref,
                 hid_ref, up_ref, down_ref, sem):
    series_here, span_slots = qkv_ref.shape[0], qkv_ref.shape[1]
    cache_slots = cache_ref.shape[1]
    width = resid_ref.shape[2]
    head_size = width // H
    up_copy = pltpu.make_async_copy(up_hbm, up_ref, sem.at[0])
    down_copy = pltpu.make_async_copy(down_hbm, down_ref, sem.at[1])
    up_copy.start()
    down_copy.start()
    group = 8 if H % 8 == 0 and (8 * head_size) % 128 == 0 else H
    group_w = group * head_size
    col_head = lax.broadcasted_iota(jnp.int32, (group, 1, group_w), 2) // head_size
    head_id = lax.broadcasted_iota(jnp.int32, (group, 1, group_w), 0)
    head_mask = col_head == head_id
    dims = (((1,), (1,)), ((), ()))
    scale = head_size ** (-0.5)
    rows = group * span_slots
    row_t = lax.broadcasted_iota(jnp.int32, (rows, span_slots), 0) % span_slots
    key_new = lax.broadcasted_iota(jnp.int32, (rows, span_slots), 1)
    key_old = lax.broadcasted_iota(jnp.int32, (rows, cache_slots), 1)
    for i in range(series_here):
        old_visible = key_old < cache_len_ref[i]
        for g in range(H // group):
            lo = g * group_w
            q = qkv_ref[i, :, lo : lo + group_w]
            k_new = qkv_ref[i, :, width + lo : width + lo + group_w]
            v_new = qkv_ref[i, :, 2 * width + lo : 2 * width + lo + group_w]
            k_old = cache_ref[i, :, lo : lo + group_w]
            v_old = cache_ref[i, :, width + lo : width + lo + group_w]
            q_heads = jnp.where(head_mask, q[None], jnp.zeros((), q.dtype)).reshape(rows, group_w)
            s_old = lax.dot_general(q_heads, k_old, dims, preferred_element_type=jnp.float32) * scale
            s_new = lax.dot_general(q_heads, k_new, dims, preferred_element_type=jnp.float32) * scale
            s_old = jnp.where(old_visible, s_old, -1e30)
            s_new = jnp.where(key_new <= row_t, s_new, -1e30)
            top = jnp.maximum(jnp.max(s_old, axis=1, keepdims=True), jnp.max(s_new, axis=1, keepdims=True))
            e_old = jnp.exp(s_old - top)
            e_new = jnp.exp(s_new - top)
            denom = jnp.sum(e_old, axis=1, keepdims=True) + jnp.sum(e_new, axis=1, keepdims=True)
            w_old = (e_old / denom).astype(jnp.bfloat16)
            w_new = (e_new / denom).astype(jnp.bfloat16)
            mixed = jnp.dot(w_old, v_old, preferred_element_type=jnp.float32) + jnp.dot(
                w_new, v_new, preferred_element_type=jnp.float32
            )
            mixed = mixed.reshape(group, span_slots, group_w)
            attended = jnp.sum(jnp.where(head_mask, mixed, 0.0), axis=0)
            hid_ref[i * span_slots : (i + 1) * span_slots, lo : lo + group_w] = (
                resid_ref[i, :, lo : lo + group_w].astype(jnp.float32) + attended
            ).astype(hid_ref.dtype)
    wide_rows = hid_ref[...].astype(jnp.float32)
    normed = (
        wide_rows
        * lax.rsqrt(jnp.mean(wide_rows * wide_rows, axis=-1, keepdims=True) + 1e-06)
        * gain_ref[...].reshape(1, width)
    ).astype(jnp.bfloat16)
    up_copy.wait()
    activated = jax.nn.silu(
        jnp.dot(normed, up_ref[...], preferred_element_type=jnp.float32)
    ).astype(jnp.bfloat16)
    down_copy.wait()
    out_ref[...] = (
        wide_rows + jnp.dot(activated, down_ref[...], preferred_element_type=jnp.float32)
    ).astype(out_ref.dtype)


def layer_block(new_qkv, cache_kv, resid, cache_len, ff_gain, w_up, w_down):
    series_here, span_slots, triple = new_qkv.shape
    width = resid.shape[2]
    vmem = pltpu.MemorySpace.VMEM if hasattr(pltpu, "MemorySpace") else pltpu.VMEM
    full = pl.BlockSpec(memory_space=vmem)
    anywhere = pl.BlockSpec(memory_space=pl.ANY)
    return pl.pallas_call(
        block_kernel,
        in_specs=[pl.BlockSpec(memory_space=pltpu.SMEM)] + [full] * 4 + [anywhere] * 2,
        out_specs=full,
        out_shape=jax.ShapeDtypeStruct((series_here * span_slots, width), jnp.bfloat16),
        scratch_shapes=[
            pltpu.VMEM((series_here * span_slots, width), jnp.bfloat16),
            pltpu.VMEM(w_up.shape, w_up.dtype),
            pltpu.VMEM(w_down.shape, w_down.dtype),
            pltpu.SemaphoreType.DMA((2,)),
        ],
    )(cache_len, new_qkv, cache_kv, resid, ff_gain, w_up, w_down)


REQ = ("y", "z", "x")
PLANE = ("z", "x")


def local(new_qkv, cache_kv, resid, span_len, cache_len, series_perm, ff_gain, w_up, w_down):
    group_size = lax.axis_size(REQ)
    me = lax.axis_index(REQ)
    plane = lax.axis_size(PLANE)
    series_here, span_slots, triple = new_qkv.shape
    width = resid.shape[2]
    layer_out = layer_block(new_qkv, cache_kv, resid, cache_len, ff_gain, w_up, w_down)
    info = jnp.concatenate(
        [jnp.broadcast_to(span_len[None], (group_size, series_here)),
         jnp.broadcast_to(series_perm[None], (group_size, series_here))], axis=1
    )
    gathered = lax.all_to_all(info, REQ, 0, 0, tiled=True)
    all_len = gathered[:, :series_here].reshape(-1)
    all_perm = gathered[:, series_here:].reshape(-1)
    series_total = all_len.shape[0]
    earlier = all_perm[None, :] < all_perm[:, None]
    all_start = jnp.sum(jnp.where(earlier, all_len[None, :], 0), axis=1)


    my_start = lax.dynamic_slice(all_start, (me * series_here,), (series_here,))
    target = jnp.arange(plane, dtype=jnp.int32)[None, :, None]
    slot = jnp.arange(span_slots, dtype=jnp.int32)[None, None, :]
    my_offset = (target - my_start[:, None, None]) % plane
    pick = (my_offset == slot) & (slot < span_len[:, None, None])
    half = width // 2
    same = jnp.arange(series_here)[:, None] == jnp.arange(series_here)[None, :]
    pick = pick.transpose(1, 0, 2)[:, :, None, :] & same[None, :, :, None]
    pick = pick.reshape(plane, series_here, 1, series_here * span_slots)
    halves = jnp.arange(2)[None, None, :, None]
    rows_here = series_here * span_slots
    placed = 0
    for h in range(2):
        pick_h = (pick & (halves == h)).reshape(-1, rows_here).astype(jnp.bfloat16)
        placed = placed + jnp.dot(
            pick_h, layer_out[:, h * half : (h + 1) * half], preferred_element_type=jnp.float32
        )
    placed = placed.astype(jnp.bfloat16)
    in_plane = lax.all_to_all(placed, PLANE, 0, 0, tiled=True)
    ys = group_size // plane
    arrived = jnp.concatenate(
        [in_plane]
        + [lax.ppermute(in_plane, "y", [(j, (j + k) % ys) for j in range(ys)]) for k in range(1, ys)],
        axis=0,
    )

    src_start = all_start.reshape(group_size, series_here)
    src_len = all_len.reshape(group_size, series_here)
    src_t = (me - src_start) % group_size
    src_row = (src_start + src_t) // group_size
    src_row = jnp.where(src_t < src_len, src_row, -1)
    src_row = src_row.reshape(ys, plane, series_here)[::-1]
    src_row = jnp.roll(src_row, lax.axis_index("y") + 1, axis=0).reshape(group_size, series_here)
    out_row = jnp.arange(rows_here, dtype=jnp.int32)[:, None, None, None]
    hit = src_row[None, :, :, None] == out_row
    result = jnp.concatenate(
        [
            jnp.dot(
                (hit & (halves.reshape(1, 1, 1, 2) == h)).reshape(rows_here, -1).astype(jnp.bfloat16),
                arrived,
                preferred_element_type=jnp.float32,
            )
            for h in range(2)
        ],
        axis=1,
    )
    return result.astype(jnp.bfloat16)


def solution(mesh):
    grp = mesh.shape["grp"]
    req = mesh.shape["req"]
    fine = jax.sharding.Mesh(mesh.devices.reshape(grp, req // 32, 8, 4), ("grp",) + REQ)
    rows = ("grp",) + REQ
    in_specs = (
        P(rows, None, None),
        P(rows, None, None),
        P(rows, None, None),
        P(rows),
        P(rows),
        P(rows),
        P(),
        P(),
        P(),
    )
    out_specs = P(rows, None)
    return jax.shard_map(local, mesh=fine, in_specs=in_specs, out_specs=out_specs, check_vma=False)
```

```python
import jax
import jax.numpy as jnp
from jax import lax
from jax.experimental import pallas as pl
from jax.experimental.pallas import tpu as pltpu
from jax.sharding import PartitionSpec as P

H = 16


def block_kernel(cache_len_ref, qkv_ref, cache_ref, resid_ref, gain_ref, up_hbm, down_hbm, out_ref,
                 hid_ref, up_ref, down_ref, sem):
    series_here, span_slots = qkv_ref.shape[0], qkv_ref.shape[1]
    cache_slots = cache_ref.shape[1]
    width = resid_ref.shape[2]
    head_size = width // H
    up_copy = pltpu.make_async_copy(up_hbm, up_ref, sem.at[0])
    down_copy = pltpu.make_async_copy(down_hbm, down_ref, sem.at[1])
    up_copy.start()
    down_copy.start()
    group = 8 if H % 8 == 0 and (8 * head_size) % 128 == 0 else H
    group_w = group * head_size
    col_head = lax.broadcasted_iota(jnp.int32, (group, 1, group_w), 2) // head_size
    head_id = lax.broadcasted_iota(jnp.int32, (group, 1, group_w), 0)
    head_mask = col_head == head_id
    dims = (((1,), (1,)), ((), ()))
    scale = head_size ** (-0.5)
    rows = group * span_slots
    row_t = lax.broadcasted_iota(jnp.int32, (rows, span_slots), 0) % span_slots
    key_new = lax.broadcasted_iota(jnp.int32, (rows, span_slots), 1)
    key_old = lax.broadcasted_iota(jnp.int32, (rows, cache_slots), 1)
    for i in range(series_here):
        old_visible = key_old < cache_len_ref[i]
        for g in range(H // group):
            lo = g * group_w
            q = qkv_ref[i, :, lo : lo + group_w]
            k_new = qkv_ref[i, :, width + lo : width + lo + group_w]
            v_new = qkv_ref[i, :, 2 * width + lo : 2 * width + lo + group_w]
            k_old = cache_ref[i, :, lo : lo + group_w]
            v_old = cache_ref[i, :, width + lo : width + lo + group_w]
            q_heads = jnp.where(head_mask, q[None], jnp.zeros((), q.dtype)).reshape(rows, group_w)
            s_old = lax.dot_general(q_heads, k_old, dims, preferred_element_type=jnp.float32) * scale
            s_new = lax.dot_general(q_heads, k_new, dims, preferred_element_type=jnp.float32) * scale
            s_old = jnp.where(old_visible, s_old, -1e30)
            s_new = jnp.where(key_new <= row_t, s_new, -1e30)
            top = jnp.maximum(jnp.max(s_old, axis=1, keepdims=True), jnp.max(s_new, axis=1, keepdims=True))
            e_old = jnp.exp(s_old - top)
            e_new = jnp.exp(s_new - top)
            denom = jnp.sum(e_old, axis=1, keepdims=True) + jnp.sum(e_new, axis=1, keepdims=True)
            w_old = (e_old / denom).astype(jnp.bfloat16)
            w_new = (e_new / denom).astype(jnp.bfloat16)
            mixed = jnp.dot(w_old, v_old, preferred_element_type=jnp.float32) + jnp.dot(
                w_new, v_new, preferred_element_type=jnp.float32
            )
            mixed = mixed.reshape(group, span_slots, group_w)
            attended = jnp.sum(jnp.where(head_mask, mixed, 0.0), axis=0)
            hid_ref[i * span_slots : (i + 1) * span_slots, lo : lo + group_w] = (
                resid_ref[i, :, lo : lo + group_w].astype(jnp.float32) + attended
            ).astype(hid_ref.dtype)
    wide_rows = hid_ref[...].astype(jnp.float32)
    normed = (
        wide_rows
        * lax.rsqrt(jnp.mean(wide_rows * wide_rows, axis=-1, keepdims=True) + 1e-06)
        * gain_ref[...].reshape(1, width)
    ).astype(jnp.bfloat16)
    up_copy.wait()
    activated = jax.nn.silu(
        jnp.dot(normed, up_ref[...], preferred_element_type=jnp.float32)
    ).astype(jnp.bfloat16)
    down_copy.wait()
    out_ref[...] = (
        wide_rows + jnp.dot(activated, down_ref[...], preferred_element_type=jnp.float32)
    ).astype(out_ref.dtype)


def layer_block(new_qkv, cache_kv, resid, cache_len, ff_gain, w_up, w_down):
    series_here, span_slots, triple = new_qkv.shape
    width = resid.shape[2]
    vmem = pltpu.MemorySpace.VMEM if hasattr(pltpu, "MemorySpace") else pltpu.VMEM
    full = pl.BlockSpec(memory_space=vmem)
    anywhere = pl.BlockSpec(memory_space=pl.ANY)
    return pl.pallas_call(
        block_kernel,
        in_specs=[pl.BlockSpec(memory_space=pltpu.SMEM)] + [full] * 4 + [anywhere] * 2,
        out_specs=full,
        out_shape=jax.ShapeDtypeStruct((series_here * span_slots, width), jnp.bfloat16),
        scratch_shapes=[
            pltpu.VMEM((series_here * span_slots, width), jnp.bfloat16),
            pltpu.VMEM(w_up.shape, w_up.dtype),
            pltpu.VMEM(w_down.shape, w_down.dtype),
            pltpu.SemaphoreType.DMA((2,)),
        ],
    )(cache_len, new_qkv, cache_kv, resid, ff_gain, w_up, w_down)


REQ = ("y", "z", "x")
PLANE = ("z", "x")


def local(new_qkv, cache_kv, resid, span_len, cache_len, series_perm, ff_gain, w_up, w_down):
    group_size = lax.axis_size(REQ)
    me = lax.axis_index(REQ)
    plane = lax.axis_size(PLANE)
    series_here, span_slots, triple = new_qkv.shape
    width = resid.shape[2]
    layer_out = layer_block(new_qkv, cache_kv, resid, cache_len, ff_gain, w_up, w_down)
    info = jnp.concatenate(
        [jnp.broadcast_to(span_len[None], (group_size, series_here)),
         jnp.broadcast_to(series_perm[None], (group_size, series_here))], axis=1
    )
    gathered = lax.all_to_all(info, REQ, 0, 0, tiled=True)
    all_len = gathered[:, :series_here].reshape(-1)
    all_perm = gathered[:, series_here:].reshape(-1)
    series_total = all_len.shape[0]
    earlier = all_perm[None, :] < all_perm[:, None]
    all_start = jnp.sum(jnp.where(earlier, all_len[None, :], 0), axis=1)


    my_start = lax.dynamic_slice(all_start, (me * series_here,), (series_here,))
    target = jnp.arange(plane, dtype=jnp.int32)[None, :, None]
    slot = jnp.arange(span_slots, dtype=jnp.int32)[None, None, :]
    my_offset = (target - my_start[:, None, None]) % plane
    pick = (my_offset == slot) & (slot < span_len[:, None, None])
    half = width // 2
    same = jnp.arange(series_here)[:, None] == jnp.arange(series_here)[None, :]
    pick = pick.transpose(1, 0, 2)[:, :, None, :] & same[None, :, :, None]
    pick = pick.reshape(plane, series_here, 1, series_here * span_slots)
    halves = jnp.arange(2)[None, None, :, None]
    rows_here = series_here * span_slots
    placed = 0
    for h in range(2):
        pick_h = (pick & (halves == h)).reshape(-1, rows_here).astype(jnp.bfloat16)
        placed = placed + jnp.dot(
            pick_h, layer_out[:, h * half : (h + 1) * half], preferred_element_type=jnp.float32
        )
    placed = placed.astype(jnp.bfloat16)
    in_plane = lax.all_to_all(placed, PLANE, 0, 0, tiled=True)
    ys = group_size // plane
    arrived = lax.all_gather(in_plane, "y", axis=0, tiled=True)

    src_start = all_start.reshape(group_size, series_here)
    src_len = all_len.reshape(group_size, series_here)
    src_t = (me - src_start) % group_size
    src_row = (src_start + src_t) // group_size
    src_row = jnp.where(src_t < src_len, src_row, -1)
    out_row = jnp.arange(rows_here, dtype=jnp.int32)[:, None, None, None]
    hit = src_row[None, :, :, None] == out_row
    result = jnp.concatenate(
        [
            jnp.dot(
                (hit & (halves.reshape(1, 1, 1, 2) == h)).reshape(rows_here, -1).astype(jnp.bfloat16),
                arrived,
                preferred_element_type=jnp.float32,
            )
            for h in range(2)
        ],
        axis=1,
    )
    return result.astype(jnp.bfloat16)


def solution(mesh):
    grp = mesh.shape["grp"]
    req = mesh.shape["req"]
    fine = jax.sharding.Mesh(mesh.devices.reshape(grp, req // 32, 8, 4), ("grp",) + REQ)
    rows = ("grp",) + REQ
    in_specs = (
        P(rows, None, None),
        P(rows, None, None),
        P(rows, None, None),
        P(rows),
        P(rows),
        P(rows),
        P(),
        P(),
        P(),
    )
    out_specs = P(rows, None)
    return jax.shard_map(local, mesh=fine, in_specs=in_specs, out_specs=out_specs, check_vma=False)
```

```python
import jax
import jax.numpy as jnp
from jax import lax
from jax.experimental import pallas as pl
from jax.experimental.pallas import tpu as pltpu
from jax.sharding import PartitionSpec as P

H = 16


def block_kernel(cache_len_ref, qkv_ref, cache_ref, resid_ref, gain_ref, up_hbm, down_hbm, out_ref,
                 hid_ref, up_ref, down_ref, sem):
    series_here, span_slots = qkv_ref.shape[0], qkv_ref.shape[1]
    cache_slots = cache_ref.shape[1]
    width = resid_ref.shape[2]
    head_size = width // H
    up_copy = pltpu.make_async_copy(up_hbm, up_ref, sem.at[0])
    down_copy = pltpu.make_async_copy(down_hbm, down_ref, sem.at[1])
    up_copy.start()
    down_copy.start()
    group = 8 if H % 8 == 0 and (8 * head_size) % 128 == 0 else H
    group_w = group * head_size
    col_head = lax.broadcasted_iota(jnp.int32, (group, 1, group_w), 2) // head_size
    head_id = lax.broadcasted_iota(jnp.int32, (group, 1, group_w), 0)
    head_mask = col_head == head_id
    dims = (((1,), (1,)), ((), ()))
    scale = head_size ** (-0.5)
    rows = group * span_slots
    row_t = lax.broadcasted_iota(jnp.int32, (rows, span_slots), 0) % span_slots
    key_new = lax.broadcasted_iota(jnp.int32, (rows, span_slots), 1)
    key_old = lax.broadcasted_iota(jnp.int32, (rows, cache_slots), 1)
    for i in range(series_here):
        old_visible = key_old < cache_len_ref[i]
        for g in range(H // group):
            lo = g * group_w
            q = qkv_ref[i, :, lo : lo + group_w]
            k_new = qkv_ref[i, :, width + lo : width + lo + group_w]
            v_new = qkv_ref[i, :, 2 * width + lo : 2 * width + lo + group_w]
            k_old = cache_ref[i, :, lo : lo + group_w]
            v_old = cache_ref[i, :, width + lo : width + lo + group_w]
            q_heads = jnp.where(head_mask, q[None], jnp.zeros((), q.dtype)).reshape(rows, group_w)
            s_old = lax.dot_general(q_heads, k_old, dims, preferred_element_type=jnp.float32) * scale
            s_new = lax.dot_general(q_heads, k_new, dims, preferred_element_type=jnp.float32) * scale
            s_old = jnp.where(old_visible, s_old, -1e30)
            s_new = jnp.where(key_new <= row_t, s_new, -1e30)
            top = jnp.maximum(jnp.max(s_old, axis=1, keepdims=True), jnp.max(s_new, axis=1, keepdims=True))
            e_old = jnp.exp(s_old - top)
            e_new = jnp.exp(s_new - top)
            denom = jnp.sum(e_old, axis=1, keepdims=True) + jnp.sum(e_new, axis=1, keepdims=True)
            w_old = (e_old / denom).astype(jnp.bfloat16)
            w_new = (e_new / denom).astype(jnp.bfloat16)
            mixed = jnp.dot(w_old, v_old, preferred_element_type=jnp.float32) + jnp.dot(
                w_new, v_new, preferred_element_type=jnp.float32
            )
            mixed = mixed.reshape(group, span_slots, group_w)
            attended = jnp.sum(jnp.where(head_mask, mixed, 0.0), axis=0)
            hid_ref[i * span_slots : (i + 1) * span_slots, lo : lo + group_w] = (
                resid_ref[i, :, lo : lo + group_w].astype(jnp.float32) + attended
            ).astype(hid_ref.dtype)
    wide_rows = hid_ref[...].astype(jnp.float32)
    normed = (
        wide_rows
        * lax.rsqrt(jnp.mean(wide_rows * wide_rows, axis=-1, keepdims=True) + 1e-06)
        * gain_ref[...].reshape(1, width)
    ).astype(jnp.bfloat16)
    up_copy.wait()
    activated = jax.nn.silu(
        jnp.dot(normed, up_ref[...], preferred_element_type=jnp.float32)
    ).astype(jnp.bfloat16)
    down_copy.wait()
    out_ref[...] = (
        wide_rows + jnp.dot(activated, down_ref[...], preferred_element_type=jnp.float32)
    ).astype(out_ref.dtype)


def layer_block(new_qkv, cache_kv, resid, cache_len, ff_gain, w_up, w_down):
    series_here, span_slots, triple = new_qkv.shape
    width = resid.shape[2]
    vmem = pltpu.MemorySpace.VMEM if hasattr(pltpu, "MemorySpace") else pltpu.VMEM
    full = pl.BlockSpec(memory_space=vmem)
    anywhere = pl.BlockSpec(memory_space=pl.ANY)
    return pl.pallas_call(
        block_kernel,
        in_specs=[pl.BlockSpec(memory_space=pltpu.SMEM)] + [full] * 4 + [anywhere] * 2,
        out_specs=full,
        out_shape=jax.ShapeDtypeStruct((series_here * span_slots, width), jnp.bfloat16),
        scratch_shapes=[
            pltpu.VMEM((series_here * span_slots, width), jnp.bfloat16),
            pltpu.VMEM(w_up.shape, w_up.dtype),
            pltpu.VMEM(w_down.shape, w_down.dtype),
            pltpu.SemaphoreType.DMA((2,)),
        ],
    )(cache_len, new_qkv, cache_kv, resid, ff_gain, w_up, w_down)


REQ = ("y", "z", "x")
PLANE = ("z", "x")


def local(new_qkv, cache_kv, resid, span_len, cache_len, series_perm, ff_gain, w_up, w_down):
    group_size = lax.axis_size(REQ)
    me = lax.axis_index(REQ)
    plane = lax.axis_size(PLANE)
    series_here, span_slots, triple = new_qkv.shape
    width = resid.shape[2]
    layer_out = layer_block(new_qkv, cache_kv, resid, cache_len, ff_gain, w_up, w_down)
    info = jnp.concatenate(
        [jnp.broadcast_to(span_len[None], (group_size, series_here)),
         jnp.broadcast_to(series_perm[None], (group_size, series_here))], axis=1
    )
    ys = group_size // plane
    in_plane_info = lax.all_to_all(info[:plane], PLANE, 0, 0, tiled=True)
    gathered = lax.all_to_all(
        jnp.broadcast_to(in_plane_info[None], (ys,) + in_plane_info.shape), "y", 0, 0, tiled=True
    ).reshape(group_size, -1)
    all_len = gathered[:, :series_here].reshape(-1)
    all_perm = gathered[:, series_here:].reshape(-1)
    series_total = all_len.shape[0]
    earlier = all_perm[None, :] < all_perm[:, None]
    all_start = jnp.sum(jnp.where(earlier, all_len[None, :], 0), axis=1)


    my_start = lax.dynamic_slice(all_start, (me * series_here,), (series_here,))
    target = jnp.arange(plane, dtype=jnp.int32)[None, :, None]
    slot = jnp.arange(span_slots, dtype=jnp.int32)[None, None, :]
    my_offset = (target - my_start[:, None, None]) % plane
    pick = (my_offset == slot) & (slot < span_len[:, None, None])
    half = width // 2
    same = jnp.arange(series_here)[:, None] == jnp.arange(series_here)[None, :]
    pick = pick.transpose(1, 0, 2)[:, :, None, :] & same[None, :, :, None]
    pick = pick.reshape(plane, series_here, 1, series_here * span_slots)
    halves = jnp.arange(2)[None, None, :, None]
    rows_here = series_here * span_slots
    placed = 0
    for h in range(2):
        pick_h = (pick & (halves == h)).reshape(-1, rows_here).astype(jnp.bfloat16)
        placed = placed + jnp.dot(
            pick_h, layer_out[:, h * half : (h + 1) * half], preferred_element_type=jnp.float32
        )
    placed = placed.astype(jnp.bfloat16)
    in_plane = lax.all_to_all(placed, PLANE, 0, 0, tiled=True)
    ys = group_size // plane
    arrived = lax.all_to_all(
        jnp.broadcast_to(in_plane[None], (ys,) + in_plane.shape), "y", 0, 0, tiled=True
    ).reshape(-1, in_plane.shape[1])

    src_start = all_start.reshape(group_size, series_here)
    src_len = all_len.reshape(group_size, series_here)
    src_t = (me - src_start) % group_size
    src_row = (src_start + src_t) // group_size
    src_row = jnp.where(src_t < src_len, src_row, -1)
    out_row = jnp.arange(rows_here, dtype=jnp.int32)[:, None, None, None]
    hit = src_row[None, :, :, None] == out_row
    result = jnp.concatenate(
        [
            jnp.dot(
                (hit & (halves.reshape(1, 1, 1, 2) == h)).reshape(rows_here, -1).astype(jnp.bfloat16),
                arrived,
                preferred_element_type=jnp.float32,
            )
            for h in range(2)
        ],
        axis=1,
    )
    return result.astype(jnp.bfloat16)


def solution(mesh):
    grp = mesh.shape["grp"]
    req = mesh.shape["req"]
    fine = jax.sharding.Mesh(mesh.devices.reshape(grp, req // 32, 8, 4), ("grp",) + REQ)
    rows = ("grp",) + REQ
    in_specs = (
        P(rows, None, None),
        P(rows, None, None),
        P(rows, None, None),
        P(rows),
        P(rows),
        P(rows),
        P(),
        P(),
        P(),
    )
    out_specs = P(rows, None)
    return jax.shard_map(local, mesh=fine, in_specs=in_specs, out_specs=out_specs, check_vma=False)
```

```python
import jax
import jax.numpy as jnp
from jax import lax
from jax.experimental import pallas as pl
from jax.experimental.pallas import tpu as pltpu
from jax.sharding import PartitionSpec as P

H = 16


def block_kernel(cache_len_ref, qkv_ref, cache_ref, resid_ref, gain_ref, up_hbm, down_hbm, out_ref,
                 hid_ref, up_ref, down_ref, sem):
    series_here, span_slots = qkv_ref.shape[0], qkv_ref.shape[1]
    cache_slots = cache_ref.shape[1]
    width = resid_ref.shape[2]
    head_size = width // H
    up_copy = pltpu.make_async_copy(up_hbm, up_ref, sem.at[0])
    down_copy = pltpu.make_async_copy(down_hbm, down_ref, sem.at[1])
    up_copy.start()
    down_copy.start()
    group = 8 if H % 8 == 0 and (8 * head_size) % 128 == 0 else H
    group_w = group * head_size
    col_head = lax.broadcasted_iota(jnp.int32, (group, 1, group_w), 2) // head_size
    head_id = lax.broadcasted_iota(jnp.int32, (group, 1, group_w), 0)
    head_mask = col_head == head_id
    dims = (((1,), (1,)), ((), ()))
    scale = head_size ** (-0.5)
    rows = group * span_slots
    row_t = lax.broadcasted_iota(jnp.int32, (rows, span_slots), 0) % span_slots
    key_new = lax.broadcasted_iota(jnp.int32, (rows, span_slots), 1)
    key_old = lax.broadcasted_iota(jnp.int32, (rows, cache_slots), 1)
    for i in range(series_here):
        old_visible = key_old < cache_len_ref[i]
        for g in range(H // group):
            lo = g * group_w
            q = qkv_ref[i, :, lo : lo + group_w]
            k_new = qkv_ref[i, :, width + lo : width + lo + group_w]
            v_new = qkv_ref[i, :, 2 * width + lo : 2 * width + lo + group_w]
            k_old = cache_ref[i, :, lo : lo + group_w]
            v_old = cache_ref[i, :, width + lo : width + lo + group_w]
            q_heads = jnp.where(head_mask, q[None], jnp.zeros((), q.dtype)).reshape(rows, group_w)
            s_old = lax.dot_general(q_heads, k_old, dims, preferred_element_type=jnp.float32) * scale
            s_new = lax.dot_general(q_heads, k_new, dims, preferred_element_type=jnp.float32) * scale
            s_old = jnp.where(old_visible, s_old, -1e30)
            s_new = jnp.where(key_new <= row_t, s_new, -1e30)
            top = jnp.maximum(jnp.max(s_old, axis=1, keepdims=True), jnp.max(s_new, axis=1, keepdims=True))
            e_old = jnp.exp(s_old - top)
            e_new = jnp.exp(s_new - top)
            denom = jnp.sum(e_old, axis=1, keepdims=True) + jnp.sum(e_new, axis=1, keepdims=True)
            w_old = (e_old / denom).astype(jnp.bfloat16)
            w_new = (e_new / denom).astype(jnp.bfloat16)
            mixed = jnp.dot(w_old, v_old, preferred_element_type=jnp.float32) + jnp.dot(
                w_new, v_new, preferred_element_type=jnp.float32
            )
            mixed = mixed.reshape(group, span_slots, group_w)
            attended = jnp.sum(jnp.where(head_mask, mixed, 0.0), axis=0)
            hid_ref[i * span_slots : (i + 1) * span_slots, lo : lo + group_w] = (
                resid_ref[i, :, lo : lo + group_w].astype(jnp.float32) + attended
            ).astype(hid_ref.dtype)
    wide_rows = hid_ref[...].astype(jnp.float32)
    normed = (
        wide_rows
        * lax.rsqrt(jnp.mean(wide_rows * wide_rows, axis=-1, keepdims=True) + 1e-06)
        * gain_ref[...].reshape(1, width)
    ).astype(jnp.bfloat16)
    up_copy.wait()
    activated = jax.nn.silu(
        jnp.dot(normed, up_ref[...], preferred_element_type=jnp.float32)
    ).astype(jnp.bfloat16)
    down_copy.wait()
    out_ref[...] = (
        wide_rows + jnp.dot(activated, down_ref[...], preferred_element_type=jnp.float32)
    ).astype(out_ref.dtype)


def layer_block(new_qkv, cache_kv, resid, cache_len, ff_gain, w_up, w_down):
    series_here, span_slots, triple = new_qkv.shape
    width = resid.shape[2]
    vmem = pltpu.MemorySpace.VMEM if hasattr(pltpu, "MemorySpace") else pltpu.VMEM
    full = pl.BlockSpec(memory_space=vmem)
    anywhere = pl.BlockSpec(memory_space=pl.ANY)
    return pl.pallas_call(
        block_kernel,
        in_specs=[pl.BlockSpec(memory_space=pltpu.SMEM)] + [full] * 4 + [anywhere] * 2,
        out_specs=full,
        out_shape=jax.ShapeDtypeStruct((series_here * span_slots, width), jnp.bfloat16),
        scratch_shapes=[
            pltpu.VMEM((series_here * span_slots, width), jnp.bfloat16),
            pltpu.VMEM(w_up.shape, w_up.dtype),
            pltpu.VMEM(w_down.shape, w_down.dtype),
            pltpu.SemaphoreType.DMA((2,)),
        ],
    )(cache_len, new_qkv, cache_kv, resid, ff_gain, w_up, w_down)


REQ = ("y", "z", "x")
PLANE = ("z", "x")


def local(new_qkv, cache_kv, resid, span_len, cache_len, series_perm, ff_gain, w_up, w_down):
    group_size = lax.axis_size(REQ)
    me = lax.axis_index(REQ)
    plane = lax.axis_size(PLANE)
    series_here, span_slots, triple = new_qkv.shape
    width = resid.shape[2]
    layer_out = layer_block(new_qkv, cache_kv, resid, cache_len, ff_gain, w_up, w_down)
    info = jnp.concatenate(
        [jnp.broadcast_to(span_len[None], (group_size, series_here)),
         jnp.broadcast_to(series_perm[None], (group_size, series_here))], axis=1
    )
    gathered = lax.all_to_all(info, REQ, 0, 0, tiled=True)
    all_len = gathered[:, :series_here].reshape(-1)
    all_perm = gathered[:, series_here:].reshape(-1)
    series_total = all_len.shape[0]
    earlier = all_perm[None, :] < all_perm[:, None]
    all_start = jnp.sum(jnp.where(earlier, all_len[None, :], 0), axis=1)


    my_start = lax.dynamic_slice(all_start, (me * series_here,), (series_here,))
    target = jnp.arange(plane, dtype=jnp.int32)[None, :, None]
    slot = jnp.arange(span_slots, dtype=jnp.int32)[None, None, :]
    my_offset = (target - my_start[:, None, None]) % plane
    pick = (my_offset == slot) & (slot < span_len[:, None, None])
    half = width // 2
    same = jnp.arange(series_here)[:, None] == jnp.arange(series_here)[None, :]
    pick = pick.transpose(1, 0, 2)[:, :, None, :] & same[None, :, :, None]
    pick = pick.reshape(plane, series_here, 1, series_here * span_slots)
    halves = jnp.arange(2)[None, None, :, None]
    rows_here = series_here * span_slots
    placed = 0
    for h in range(2):
        pick_h = (pick & (halves == h)).reshape(-1, rows_here).astype(jnp.bfloat16)
        placed = placed + jnp.dot(
            pick_h, layer_out[:, h * half : (h + 1) * half], preferred_element_type=jnp.float32
        )
    placed = placed.astype(jnp.bfloat16)
    in_plane = lax.all_to_all(placed, PLANE, 0, 0, tiled=True)
    ys = group_size // plane
    in_plane = in_plane.reshape(-1, width)
    arrived = lax.all_to_all(
        jnp.broadcast_to(in_plane[None], (ys,) + in_plane.shape), "y", 0, 0, tiled=True
    ).reshape(-1, width)

    src_start = all_start.reshape(group_size, series_here)
    src_len = all_len.reshape(group_size, series_here)
    src_t = (me - src_start) % group_size
    src_row = (src_start + src_t) // group_size
    src_row = jnp.where(src_t < src_len, src_row, -1)
    out_row = jnp.arange(rows_here, dtype=jnp.int32)[:, None]
    gather = (src_row.reshape(1, -1) == out_row).astype(jnp.bfloat16)
    result = jnp.dot(gather, arrived, preferred_element_type=jnp.float32)
    return result.astype(jnp.bfloat16)


def solution(mesh):
    grp = mesh.shape["grp"]
    req = mesh.shape["req"]
    fine = jax.sharding.Mesh(mesh.devices.reshape(grp, req // 32, 8, 4), ("grp",) + REQ)
    rows = ("grp",) + REQ
    in_specs = (
        P(rows, None, None),
        P(rows, None, None),
        P(rows, None, None),
        P(rows),
        P(rows),
        P(rows),
        P(),
        P(),
        P(),
    )
    out_specs = P(rows, None)
    return jax.shard_map(local, mesh=fine, in_specs=in_specs, out_specs=out_specs, check_vma=False)
```
